32 devices in a mesh: grid: 8 (over y, x, core), head: 4 (over z).
Axes of the slice: x: 2, y: 2, z: 4, core: 2. Of those that a mesh axis runs over, the one named last changes fastest.
Arguments:
- queries: bfloat16 [32768, 1024], P('grid', 'head'), may hold values from -12 to 12
- resid: bfloat16 [32768, 1024], P('grid', 'head'), may hold values from -6 to 6
- keys: bfloat16 [49152, 1024], P('grid', 'head'), may hold values from -6 to 6
- values: bfloat16 [49152, 1024], P('grid', 'head'), may hold values from -6 to 6
- w_out: bfloat16 [1024, 1024], replicated, may hold values from -0.75 to 0.75
- block_lists: int32 [256, 12], P('grid'), may hold values from 0 to 383, as said below
- block_counts: int32 [256], P('grid'), may hold values from 1 to 12, as said below
Outputs:
- mixed: bfloat16 [32768, 1024], P('grid', 'head')
The draws below stay inside these ranges and needn't reach their ends.
Inputs may be any that keep to these rules, and one draw needn't show every extreme that they name: `block_lists`: each row lists 12 different latent blocks. The blocks listed for grid blocks of the g-th 4096 grid points lie in latent blocks (g - 1) * 48 to (g + 2) * 48 - 1. `block_counts`: entries of a list at positions not below the count are not used.
All inputs are finite; a program needn't handle non-finite values.
Results may differ from the reference program's by a relative error of at most 0.005.
Values may be sent and summed in bfloat16 or wider, within the bound.
No kernel may reach another device: no remote copies, remote signals or barrier semaphores. Data moves between devices by JAX's collectives and lax.ppermute only.
A program may use at most 128 MiB of HBM per device.

```python
import math
import jax
import jax.numpy as jnp
from jax import lax

D = 1024
HEADS = 16
BLK = 128
SLOTS = 12
ROWS_DEV = 4096
LB_DEV = 48
GRID = 32768
GBLOCKS = 256
LBLOCKS = 384
LATENT = 49152
N_GRID = 8


def pattern_lists(key):
    base = jax.random.fold_in(key, 11)
    rows = jnp.arange(GBLOCKS, dtype=jnp.int32)
    per_dev = ROWS_DEV // BLK
    owner = rows // per_dev
    center = owner * LB_DEV + rows % per_dev * LB_DEV // per_dev
    low = jnp.clip(center - LB_DEV, 0, LB_DEV * N_GRID - 2 * LB_DEV)
    width = 2 * LB_DEV
    perms = jax.vmap(lambda k: jax.random.permutation(k, width))(jax.random.split(base, GBLOCKS))
    target = jnp.where(rows % 2 == 0, 0, width - 1)
    place = jnp.argmax(perms == target[:, None], axis=1)
    turned = jax.vmap(lambda p, s: jnp.roll(p, -s))(perms, place)
    return (low[:, None] + turned[:, :SLOTS]).astype(jnp.int32)


def latent_keys(key):
    base = jax.random.fold_in(key, 23)
    return jnp.clip(jax.random.normal(base, (LATENT, D), jnp.float32), -6.0, 6.0)


def draw_keys(key, part):
    return latent_keys(key).astype(jnp.bfloat16)


def draw_queries(key, part):
    base = jax.random.fold_in(key, 31)
    return jnp.clip(2.0 * jax.random.normal(base, (GRID, D), jnp.float32), -12.0, 12.0).astype(jnp.bfloat16)


def draw_block_lists(key, part):
    return pattern_lists(key)


def draw_block_counts(key, part):
    base = jax.random.fold_in(key, 47)
    rows = jnp.arange(GBLOCKS, dtype=jnp.int32)
    owner = rows // (ROWS_DEV // BLK)
    polar = (owner < N_GRID // 4) | (owner >= N_GRID - N_GRID // 4)
    lowest = jnp.where(polar, SLOTS // 2, 1)
    drawn = jax.random.randint(base, (GBLOCKS,), lowest, SLOTS + 1)
    drawn = jnp.where(rows % 8 == 0, SLOTS, drawn)
    drawn = jnp.where((rows % 8 == 4) & jnp.logical_not(polar), 1, drawn)
    return drawn.astype(jnp.int32)


def block_levels(key, dims, shards, least, top_value):
    gain, own = 1.0, jax.random.fold_in(key, 6)
    for dim, shards_of in shards:
        steps = jnp.exp(jax.random.uniform(jax.random.fold_in(own, dim), (shards_of,), jnp.float32, least / len(shards), top_value / len(shards)))
        gain = gain * jnp.repeat(steps, dims[dim] // shards_of).reshape([-1 if axis == dim else 1 for axis in range(len(dims))])
    return gain


def scatter_about(rng, shape, spread, bound, cuts=(), kind=jnp.bfloat16):
    entries = jax.random.normal(rng, shape, jnp.float32) * spread
    if len(cuts) > 0:
        entries = block_levels(rng, shape, cuts, -0.22, 0.18) * entries
    return jnp.clip(entries, min=-bound, max=bound).astype(kind)


def setup_inputs(seed: int = 0) -> dict:
    seeds = jax.random.split(jax.random.key(seed), 8)
    queries = draw_queries(jax.random.fold_in(seeds[7], 71), 0)
    resid = scatter_about(seeds[1], (GRID, D), 1.0, 6.0, ((0, 8), (1, 4)))
    keys = draw_keys(jax.random.fold_in(seeds[7], 71), 0)
    values = scatter_about(seeds[3], (LATENT, D), 1.0, 6.0, ((0, 8), (1, 4)))
    w_out = scatter_about(seeds[4], (D, D), (D // 16) ** -0.5, 0.75)
    block_lists = draw_block_lists(jax.random.fold_in(seeds[7], 71), 0)
    block_counts = draw_block_counts(jax.random.fold_in(seeds[7], 71), 0)
    return {"queries": queries, "resid": resid, "keys": keys, "values": values, "w_out": w_out, "block_lists": block_lists, "block_counts": block_counts}


def reference(queries, resid, keys, values, w_out, block_lists, block_counts):
    head_dim = D // HEADS
    scale = 1.0 / math.sqrt(head_dim)
    key_tiles = keys.reshape(LBLOCKS, BLK, D)
    value_tiles = values.reshape(LBLOCKS, BLK, D)

    def one_block(index):
        start = (index * BLK).astype(jnp.int32)
        block_q = lax.dynamic_slice_in_dim(queries, start, BLK, 0).astype(jnp.float32).reshape(BLK, HEADS, head_dim)
        listed = block_lists[index]
        block_k = key_tiles[listed].reshape(SLOTS * BLK, HEADS, head_dim).astype(jnp.float32)
        block_v = value_tiles[listed].reshape(SLOTS * BLK, HEADS, head_dim).astype(jnp.float32)
        live = jnp.arange(SLOTS, dtype=jnp.int32) < block_counts[index]
        usable = jnp.broadcast_to(live[:, None], (SLOTS, BLK)).reshape(SLOTS * BLK)
        score = jnp.einsum('qhd,khd->hqk', block_q, block_k) * scale
        score = jnp.where(usable[None, None, :], score, -1e+30)
        top = lax.optimization_barrier(jnp.max(score, axis=-1, keepdims=True))
        weight = jnp.exp(score - top)
        total = lax.optimization_barrier(jnp.sum(weight, axis=-1, keepdims=True))
        weight_low = weight.astype(jnp.bfloat16).astype(jnp.float32)
        summed = jnp.einsum('hqk,khd->hqd', weight_low, block_v) / total
        return jnp.transpose(summed, (1, 0, 2)).reshape(BLK, D).astype(jnp.bfloat16)
    attended = lax.map(one_block, jnp.arange(GBLOCKS, dtype=jnp.int32)).reshape(GRID, D)
    projected = jnp.dot(attended, w_out, preferred_element_type=jnp.float32)
    return (resid.astype(jnp.float32) + projected).astype(jnp.bfloat16)
```

```python
import functools
import math

import jax
import jax.numpy as jnp
from jax import lax
from jax.experimental import pallas as pl
from jax.experimental.pallas import tpu as pltpu
from jax.sharding import PartitionSpec as P

D = 1024
HEADS = 16
BLK = 128


def halos(cells, axis):
    count = lax.axis_size(axis)
    from_left = lax.ppermute(cells, axis, [(i, i + 1) for i in range(count - 1)])
    from_right = lax.ppermute(cells, axis, [(i + 1, i) for i in range(count - 1)])
    return from_left, from_right


def attend_kernel(heads_here, head_dim, per_device, ids_ref, counts_ref, q_ref,
                  k_left, k_own, k_right, v_left, v_own, v_right,
                  o_ref, stacked, kbuf, vbuf, acc, top, total):
    b = pl.program_id(0)
    slots = ids_ref.shape[0] // counts_ref.shape[0]
    rows, width = q_ref.shape
    scale = 1.0 / math.sqrt(head_dim)
    column_head = lax.broadcasted_iota(jnp.int32, (rows, width), 1) // head_dim
    q = q_ref[...]
    for h in range(heads_here):
        stacked[h * rows:(h + 1) * rows, :] = jnp.where(column_head == h, q, jnp.zeros_like(q))
    acc[...] = jnp.zeros_like(acc)
    top[...] = jnp.full_like(top, -jnp.inf)
    total[...] = jnp.zeros_like(total)
    sources = ((k_left, v_left), (k_own, v_own), (k_right, v_right))

    def step(j, carry):
        index = ids_ref[b * slots + j]
        source = index // per_device
        block = index % per_device
        for s, (k_ref, v_ref) in enumerate(sources):
            @pl.when(source == s)
            def _():
                kbuf[...] = k_ref[block]
                vbuf[...] = v_ref[block]

        score = lax.dot_general(
            stacked[...], kbuf[...], (((1,), (1,)), ((), ())),
            preferred_element_type=jnp.float32,
        ) * scale
        previous = top[...]
        new_top = jnp.maximum(previous, jnp.max(score, axis=1, keepdims=True))
        rescale = jnp.exp(previous - new_top)
        weight = jnp.exp(score - new_top)
        total[...] = rescale * total[...] + jnp.sum(weight, axis=1, keepdims=True)
        acc[...] = rescale * acc[...] + jnp.dot(
            weight.astype(jnp.bfloat16), vbuf[...], preferred_element_type=jnp.float32
        )
        top[...] = new_top
        return carry

    lax.fori_loop(0, counts_ref[b], step, 0)
    out = jnp.zeros((rows, width), jnp.float32)
    for h in range(heads_here):
        part = acc[h * rows:(h + 1) * rows, :] / total[h * rows:(h + 1) * rows, :]
        out = jnp.where(column_head == h, part, out)
    o_ref[...] = out.astype(o_ref.dtype)


def attend(queries, keys, values, first_block, block_lists, block_counts):
    rows, width = queries.shape
    head_dim = D // HEADS
    heads_here = width // head_dim
    per_device = keys.shape[0] // BLK
    slots = block_lists.shape[1]
    gblocks = rows // BLK
    k_left, k_right = halos(keys, "grid")
    v_left, v_right = halos(values, "grid")
    tiles = [a.reshape(per_device, BLK, width) for a in (k_left, keys, k_right, v_left, values, v_right)]
    ids = jnp.clip(block_lists - first_block, 0, 3 * per_device - 1).reshape(-1).astype(jnp.int32)
    counts = block_counts.astype(jnp.int32)
    whole = pl.BlockSpec(memory_space=pltpu.VMEM)
    kernel = functools.partial(attend_kernel, heads_here, head_dim, per_device)
    return pl.pallas_call(
        kernel,
        out_shape=jax.ShapeDtypeStruct((rows, width), jnp.bfloat16),
        grid_spec=pltpu.PrefetchScalarGridSpec(
            num_scalar_prefetch=2,
            grid=(gblocks,),
            in_specs=[pl.BlockSpec((BLK, width), lambda b, ids, counts: (b, 0))] + [whole] * 6,
            out_specs=pl.BlockSpec((BLK, width), lambda b, ids, counts: (b, 0)),
            scratch_shapes=[
                pltpu.VMEM((heads_here * BLK, width), jnp.bfloat16),
                pltpu.VMEM((BLK, width), jnp.bfloat16),
                pltpu.VMEM((BLK, width), jnp.bfloat16),
                pltpu.VMEM((heads_here * BLK, width), jnp.float32),
                pltpu.VMEM((heads_here * BLK, 1), jnp.float32),
                pltpu.VMEM((heads_here * BLK, 1), jnp.float32),
            ],
        ),
        compiler_params=pltpu.CompilerParams(
            dimension_semantics=("arbitrary",),
            vmem_limit_bytes=48 * 1024 * 1024,
        ),
        cost_estimate=pl.CostEstimate(
            flops=4 * gblocks * slots * heads_here * BLK * BLK * width,
            transcendentals=gblocks * slots * heads_here * BLK * BLK,
            bytes_accessed=2 * (3 * rows * width + 6 * keys.size),
        ),
    )(ids, counts, queries, *tiles)


def local(queries, resid, keys, values, w_out, block_lists, block_counts):
    per_device = keys.shape[0] // BLK
    first_block = (lax.axis_index("grid") - 1) * per_device
    attended = attend(queries, keys, values, first_block, block_lists, block_counts)
    arrived = lax.all_to_all(attended, "head", split_axis=0, concat_axis=1, tiled=True)
    projected = jnp.dot(arrived, w_out, preferred_element_type=jnp.float32)
    returned = lax.all_to_all(projected, "head", split_axis=1, concat_axis=0, tiled=True)
    return (resid.astype(jnp.float32) + returned).astype(jnp.bfloat16)


def solution(mesh):
    placed = (
        P("grid", "head"),
        P("grid", "head"),
        P("grid", "head"),
        P("grid", "head"),
        P(),
        P("grid", None),
        P("grid"),
    )
    return jax.shard_map(
        local, mesh=mesh, in_specs=placed, out_specs=P("grid", "head"), check_vma=False
    )
```

```python
import functools
import math

import jax
import jax.numpy as jnp
from jax import lax
from jax.experimental import pallas as pl
from jax.experimental.pallas import tpu as pltpu
from jax.sharding import PartitionSpec as P

D = 1024
HEADS = 16
BLK = 128


def halos(cells, axis):
    count = lax.axis_size(axis)
    from_left = lax.ppermute(cells, axis, [(i, i + 1) for i in range(count - 1)])
    from_right = lax.ppermute(cells, axis, [(i + 1, i) for i in range(count - 1)])
    return from_left, from_right


def attend_kernel(heads_here, head_dim, per_device, ids_ref, counts_ref, q_ref,
                  k_left, k_own, k_right, v_left, v_own, v_right,
                  o_ref, stacked, kbuf, vbuf, blockdiag, scores, running, spread, summed):
    b = pl.program_id(0)
    slots = ids_ref.shape[0] // counts_ref.shape[0]
    rows, width = q_ref.shape
    scale = 1.0 / math.sqrt(head_dim)
    column_head = lax.broadcasted_iota(jnp.int32, (rows, width), 1) // head_dim
    q = q_ref[...]
    for h in range(heads_here):
        stacked[h * rows:(h + 1) * rows, :] = jnp.where(column_head == h, q, jnp.zeros_like(q))
    running[...] = jnp.full_like(running, -jnp.inf)
    summed[...] = jnp.zeros_like(summed)
    sources = ((k_left, v_left), (k_own, v_own), (k_right, v_right))
    count = counts_ref[b]

    def fetch(j, buf, which):
        index = ids_ref[b * slots + j]
        source = index // per_device
        block = index % per_device
        for s, refs in enumerate(sources):
            @pl.when(source == s)
            def _():
                buf[...] = refs[which][block]

    def score_step(j, carry):
        fetch(j, kbuf, 0)
        score = lax.dot_general(
            stacked[...], kbuf[...], (((1,), (1,)), ((), ())),
            preferred_element_type=jnp.float32,
        ) * scale
        scores[j] = score
        running[...] = jnp.maximum(running[...], score)
        return carry

    lax.fori_loop(0, count, score_step, 0)
    spread[...] = jnp.broadcast_to(jnp.max(running[...], axis=1, keepdims=True), spread.shape)

    def weight_step(j, acc):
        fetch(j, vbuf, 1)
        weight = jnp.exp(scores[j] - spread[...])
        summed[...] += weight
        low = weight.astype(jnp.bfloat16)
        side = jnp.concatenate([low[h * rows:(h + 1) * rows, :] for h in range(heads_here)], axis=1)
        v = vbuf[...]
        for h in range(heads_here):
            blockdiag[h * rows:(h + 1) * rows, :] = jnp.where(column_head == h, v, jnp.zeros_like(v))
        return acc + jnp.dot(side, blockdiag[...], preferred_element_type=jnp.float32)

    acc = lax.fori_loop(0, count, weight_step, jnp.zeros((rows, width), jnp.float32))
    total = jnp.sum(summed[...], axis=1, keepdims=True)
    out = jnp.zeros((rows, width), jnp.float32)
    for h in range(heads_here):
        out = jnp.where(column_head == h, acc / total[h * rows:(h + 1) * rows, :], out)
    o_ref[...] = out.astype(o_ref.dtype)


def attend(queries, keys, values, first_block, block_lists, block_counts):
    rows, width = queries.shape
    head_dim = D // HEADS
    heads_here = width // head_dim
    per_device = keys.shape[0] // BLK
    slots = block_lists.shape[1]
    gblocks = rows // BLK
    k_left, k_right = halos(keys, "grid")
    v_left, v_right = halos(values, "grid")
    tiles = [a.reshape(per_device, BLK, width) for a in (k_left, keys, k_right, v_left, values, v_right)]
    ids = jnp.clip(block_lists - first_block, 0, 3 * per_device - 1).reshape(-1).astype(jnp.int32)
    counts = block_counts.astype(jnp.int32)
    whole = pl.BlockSpec(
        (per_device, BLK, width), lambda b, ids, counts: (0, 0, 0), pipeline_mode=pl.Buffered(1)
    )
    kernel = functools.partial(attend_kernel, heads_here, head_dim, per_device)
    return pl.pallas_call(
        kernel,
        out_shape=jax.ShapeDtypeStruct((rows, width), jnp.bfloat16),
        grid_spec=pltpu.PrefetchScalarGridSpec(
            num_scalar_prefetch=2,
            grid=(gblocks,),
            in_specs=[pl.BlockSpec((BLK, width), lambda b, ids, counts: (b, 0))] + [whole] * 6,
            out_specs=pl.BlockSpec((BLK, width), lambda b, ids, counts: (b, 0)),
            scratch_shapes=[
                pltpu.VMEM((heads_here * BLK, width), jnp.bfloat16),
                pltpu.VMEM((BLK, width), jnp.bfloat16),
                pltpu.VMEM((BLK, width), jnp.bfloat16),
                pltpu.VMEM((heads_here * BLK, width), jnp.bfloat16),
                pltpu.VMEM((slots, heads_here * BLK, BLK), jnp.float32),
                pltpu.VMEM((heads_here * BLK, BLK), jnp.float32),
                pltpu.VMEM((heads_here * BLK, BLK), jnp.float32),
                pltpu.VMEM((heads_here * BLK, BLK), jnp.float32),
            ],
        ),
        compiler_params=pltpu.CompilerParams(
            dimension_semantics=("arbitrary",),
            vmem_limit_bytes=48 * 1024 * 1024,
        ),
        cost_estimate=pl.CostEstimate(
            flops=4 * gblocks * slots * heads_here * BLK * BLK * width,
            transcendentals=gblocks * slots * heads_here * BLK * BLK,
            bytes_accessed=2 * (3 * rows * width + 6 * keys.size),
        ),
    )(ids, counts, queries, *tiles)


def local(queries, resid, keys, values, w_out, block_lists, block_counts):
    per_device = keys.shape[0] // BLK
    first_block = (lax.axis_index("grid") - 1) * per_device
    attended = attend(queries, keys, values, first_block, block_lists, block_counts)
    arrived = lax.all_to_all(attended, "head", split_axis=0, concat_axis=1, tiled=True)
    projected = jnp.dot(arrived, w_out, preferred_element_type=jnp.float32)
    returned = lax.all_to_all(projected, "head", split_axis=1, concat_axis=0, tiled=True)
    return (resid.astype(jnp.float32) + returned).astype(jnp.bfloat16)


def solution(mesh):
    placed = (
        P("grid", "head"),
        P("grid", "head"),
        P("grid", "head"),
        P("grid", "head"),
        P(),
        P("grid", None),
        P("grid"),
    )
    return jax.shard_map(
        local, mesh=mesh, in_specs=placed, out_specs=P("grid", "head"), check_vma=False
    )
```

```python
import functools
import math

import jax
import jax.numpy as jnp
from jax import lax
from jax.experimental import pallas as pl
from jax.experimental.pallas import tpu as pltpu
from jax.sharding import PartitionSpec as P

D = 1024
HEADS = 16
BLK = 128


def halos(cells, axis):
    count = lax.axis_size(axis)
    from_left = lax.ppermute(cells, axis, [(i, i + 1) for i in range(count - 1)])
    from_right = lax.ppermute(cells, axis, [(i + 1, i) for i in range(count - 1)])
    return from_left, from_right


def attend_kernel(heads_here, head_dim, per_device, ids_ref, counts_ref, q_ref,
                  k_left, k_own, k_right, v_left, v_own, v_right,
                  o_ref, stacked, kbuf, vbuf, blockdiag, scores, running, spread, summed):
    b = pl.program_id(0)
    slots = ids_ref.shape[0] // counts_ref.shape[0]
    rows, width = q_ref.shape
    scale = 1.0 / math.sqrt(head_dim)
    column_head = lax.broadcasted_iota(jnp.int32, (rows, width), 1) // head_dim
    q = q_ref[...]
    for h in range(heads_here):
        stacked[h * rows:(h + 1) * rows, :] = jnp.where(column_head == h, q, jnp.zeros_like(q))
    running[...] = jnp.full_like(running, -jnp.inf)
    summed[...] = jnp.zeros_like(summed)
    sources = ((k_left, v_left), (k_own, v_own), (k_right, v_right))
    count = counts_ref[b]

    def fetch(j, buf, which):
        index = ids_ref[b * slots + j]
        source = index // per_device
        block = index % per_device
        for s, refs in enumerate(sources):
            @pl.when(source == s)
            def _():
                buf[...] = refs[which][block]

    def score_step(j, carry):
        fetch(j, kbuf, 0)
        score = lax.dot_general(
            stacked[...], kbuf[...], (((1,), (1,)), ((), ())),
            preferred_element_type=jnp.float32,
        ) * scale
        scores[j] = score
        running[...] = jnp.maximum(running[...], score)
        return carry

    lax.fori_loop(0, count, score_step, 0)
    spread[...] = jnp.broadcast_to(jnp.max(running[...], axis=1, keepdims=True), spread.shape)

    def weight_step(j, acc):
        fetch(j, vbuf, 1)
        weight = jnp.exp(scores[j] - spread[...])
        summed[...] += weight
        low = weight.astype(jnp.bfloat16)
        side = jnp.concatenate([low[h * rows:(h + 1) * rows, :] for h in range(heads_here)], axis=1)
        v = vbuf[...]
        for h in range(heads_here):
            blockdiag[h * rows:(h + 1) * rows, :] = jnp.where(column_head == h, v, jnp.zeros_like(v))
        return acc + jnp.dot(side, blockdiag[...], preferred_element_type=jnp.float32)

    acc = lax.fori_loop(0, count, weight_step, jnp.zeros((rows, width), jnp.float32))
    total = jnp.sum(summed[...], axis=1, keepdims=True)
    out = jnp.zeros((rows, width), jnp.float32)
    for h in range(heads_here):
        out = jnp.where(column_head == h, acc / total[h * rows:(h + 1) * rows, :], out)
    o_ref[...] = out.astype(o_ref.dtype)


def attend(queries, keys, values, first_block, block_lists, block_counts):
    rows, width = queries.shape
    head_dim = D // HEADS
    heads_here = width // head_dim
    per_device = keys.shape[0] // BLK
    slots = block_lists.shape[1]
    gblocks = rows // BLK
    k_left, k_right = halos(keys, "grid")
    v_left, v_right = halos(values, "grid")
    tiles = [a.reshape(per_device, BLK, width) for a in (k_left, keys, k_right, v_left, values, v_right)]
    ids = jnp.clip(block_lists - first_block, 0, 3 * per_device - 1).reshape(-1).astype(jnp.int32)
    counts = block_counts.astype(jnp.int32)
    whole = pl.BlockSpec(
        (per_device, BLK, width), lambda b, ids, counts: (0, 0, 0), pipeline_mode=pl.Buffered(1)
    )
    kernel = functools.partial(attend_kernel, heads_here, head_dim, per_device)
    return pl.pallas_call(
        kernel,
        out_shape=jax.ShapeDtypeStruct((rows, width), jnp.bfloat16),
        grid_spec=pltpu.PrefetchScalarGridSpec(
            num_scalar_prefetch=2,
            grid=(gblocks,),
            in_specs=[pl.BlockSpec((BLK, width), lambda b, ids, counts: (b, 0))] + [whole] * 6,
            out_specs=pl.BlockSpec((BLK, width), lambda b, ids, counts: (b, 0)),
            scratch_shapes=[
                pltpu.VMEM((heads_here * BLK, width), jnp.bfloat16),
                pltpu.VMEM((BLK, width), jnp.bfloat16),
                pltpu.VMEM((BLK, width), jnp.bfloat16),
                pltpu.VMEM((heads_here * BLK, width), jnp.bfloat16),
                pltpu.VMEM((slots, heads_here * BLK, BLK), jnp.float32),
                pltpu.VMEM((heads_here * BLK, BLK), jnp.float32),
                pltpu.VMEM((heads_here * BLK, BLK), jnp.float32),
                pltpu.VMEM((heads_here * BLK, BLK), jnp.float32),
            ],
        ),
        compiler_params=pltpu.CompilerParams(
            dimension_semantics=("arbitrary",),
            vmem_limit_bytes=48 * 1024 * 1024,
        ),
        cost_estimate=pl.CostEstimate(
            flops=4 * gblocks * slots * heads_here * BLK * BLK * width,
            transcendentals=gblocks * slots * heads_here * BLK * BLK,
            bytes_accessed=2 * (3 * rows * width + 6 * keys.size),
        ),
    )(ids, counts, queries, *tiles)


def local(queries, resid, keys, values, w_out, block_lists, block_counts):
    per_device = keys.shape[0] // BLK
    first_block = (lax.axis_index("grid") - 1) * per_device
    attended = attend(queries, keys, values, first_block, block_lists, block_counts)
    width = resid.shape[1]
    gathered = lax.all_gather(attended, "head", axis=1, tiled=True)
    columns = lax.dynamic_slice_in_dim(w_out, lax.axis_index("head") * width, width, axis=1)
    projected = jnp.dot(gathered, columns, preferred_element_type=jnp.float32)
    return (resid.astype(jnp.float32) + projected).astype(jnp.bfloat16)


def solution(mesh):
    placed = (
        P("grid", "head"),
        P("grid", "head"),
        P("grid", "head"),
        P("grid", "head"),
        P(),
        P("grid", None),
        P("grid"),
    )
    return jax.shard_map(
        local, mesh=mesh, in_specs=placed, out_specs=P("grid", "head"), check_vma=False
    )
```

```python
import functools
import math

import jax
import jax.numpy as jnp
from jax import lax
from jax.experimental import pallas as pl
from jax.experimental.pallas import tpu as pltpu
from jax.sharding import PartitionSpec as P

D = 1024
HEADS = 16
BLK = 128


def halos(cells, axis):
    count = lax.axis_size(axis)
    from_left = lax.ppermute(cells, axis, [(i, i + 1) for i in range(count - 1)])
    from_right = lax.ppermute(cells, axis, [(i + 1, i) for i in range(count - 1)])
    return from_left, from_right


def attend_kernel(heads_here, head_dim, per_device, ids_ref, counts_ref, q_ref,
                  k_left, k_own, k_right, v_left, v_own, v_right,
                  o_ref, stacked, kbuf, vbuf, blockdiag, scores, running, spread, summed):
    b = pl.program_id(0)
    slots = ids_ref.shape[0] // counts_ref.shape[0]
    rows, width = q_ref.shape
    scale = 1.0 / math.sqrt(head_dim)
    column_head = lax.broadcasted_iota(jnp.int32, (rows, width), 1) // head_dim
    q = q_ref[...]
    for h in range(heads_here):
        stacked[h * rows:(h + 1) * rows, :] = jnp.where(column_head == h, q, jnp.zeros_like(q))
    running[...] = jnp.full_like(running, -jnp.inf)
    summed[...] = jnp.zeros_like(summed)
    sources = ((k_left, v_left), (k_own, v_own), (k_right, v_right))
    count = counts_ref[b]

    def fetch(j, buf, which):
        index = ids_ref[b * slots + j]
        source = index // per_device
        block = index % per_device
        for s, refs in enumerate(sources):
            @pl.when(source == s)
            def _():
                buf[...] = refs[which][block]

    def score_step(j, carry):
        fetch(j, kbuf, 0)
        score = lax.dot_general(
            stacked[...], kbuf[...], (((1,), (1,)), ((), ())),
            preferred_element_type=jnp.float32,
        ) * scale
        scores[j] = score
        running[...] = jnp.maximum(running[...], score)
        return carry

    lax.fori_loop(0, count, score_step, 0)
    spread[...] = jnp.broadcast_to(jnp.max(running[...], axis=1, keepdims=True), spread.shape)

    def weight_step(j, acc):
        fetch(j, vbuf, 1)
        weight = jnp.exp(scores[j] - spread[...])
        summed[...] += weight
        low = weight.astype(jnp.bfloat16)
        side = jnp.concatenate([low[h * rows:(h + 1) * rows, :] for h in range(heads_here)], axis=1)
        v = vbuf[...]
        for h in range(heads_here):
            blockdiag[h * rows:(h + 1) * rows, :] = jnp.where(column_head == h, v, jnp.zeros_like(v))
        return acc + jnp.dot(side, blockdiag[...], preferred_element_type=jnp.float32)

    acc = lax.fori_loop(0, count, weight_step, jnp.zeros((rows, width), jnp.float32))
    total = jnp.sum(summed[...], axis=1, keepdims=True)
    out = jnp.zeros((rows, width), jnp.float32)
    for h in range(heads_here):
        out = jnp.where(column_head == h, acc / total[h * rows:(h + 1) * rows, :], out)
    o_ref[...] = out.astype(o_ref.dtype)


def attend(queries, keys, values, first_block, block_lists, block_counts):
    rows, width = queries.shape
    head_dim = D // HEADS
    heads_here = width // head_dim
    per_device = keys.shape[0] // BLK
    slots = block_lists.shape[1]
    gblocks = rows // BLK
    k_left, k_right = halos(keys, "grid")
    v_left, v_right = halos(values, "grid")
    tiles = [a.reshape(per_device, BLK, width) for a in (k_left, keys, k_right, v_left, values, v_right)]
    ids = jnp.clip(block_lists - first_block, 0, 3 * per_device - 1).reshape(-1).astype(jnp.int32)
    counts = block_counts.astype(jnp.int32)
    whole = pl.BlockSpec(
        (per_device, BLK, width), lambda b, ids, counts: (0, 0, 0), pipeline_mode=pl.Buffered(1)
    )
    kernel = functools.partial(attend_kernel, heads_here, head_dim, per_device)
    return pl.pallas_call(
        kernel,
        out_shape=jax.ShapeDtypeStruct((rows, width), jnp.bfloat16),
        grid_spec=pltpu.PrefetchScalarGridSpec(
            num_scalar_prefetch=2,
            grid=(gblocks,),
            in_specs=[pl.BlockSpec((BLK, width), lambda b, ids, counts: (b, 0))] + [whole] * 6,
            out_specs=pl.BlockSpec((BLK, width), lambda b, ids, counts: (b, 0)),
            scratch_shapes=[
                pltpu.VMEM((heads_here * BLK, width), jnp.bfloat16),
                pltpu.VMEM((BLK, width), jnp.bfloat16),
                pltpu.VMEM((BLK, width), jnp.bfloat16),
                pltpu.VMEM((heads_here * BLK, width), jnp.bfloat16),
                pltpu.VMEM((slots, heads_here * BLK, BLK), jnp.float32),
                pltpu.VMEM((heads_here * BLK, BLK), jnp.float32),
                pltpu.VMEM((heads_here * BLK, BLK), jnp.float32),
                pltpu.VMEM((heads_here * BLK, BLK), jnp.float32),
            ],
        ),
        compiler_params=pltpu.CompilerParams(
            dimension_semantics=("arbitrary",),
            vmem_limit_bytes=48 * 1024 * 1024,
        ),
        cost_estimate=pl.CostEstimate(
            flops=4 * gblocks * slots * heads_here * BLK * BLK * width,
            transcendentals=gblocks * slots * heads_here * BLK * BLK,
            bytes_accessed=2 * (3 * rows * width + 6 * keys.size),
        ),
    )(ids, counts, queries, *tiles)


def local(queries, resid, keys, values, w_out, block_lists, block_counts):
    per_device = keys.shape[0] // BLK
    first_block = (lax.axis_index("grid") - 1) * per_device
    attended = attend(queries, keys, values, first_block, block_lists, block_counts)
    arrived = lax.all_to_all(attended, "head", split_axis=0, concat_axis=1, tiled=True)
    projected = jnp.dot(arrived, w_out, preferred_element_type=jnp.float32).astype(jnp.bfloat16)
    returned = lax.all_to_all(projected, "head", split_axis=1, concat_axis=0, tiled=True)
    return (resid.astype(jnp.float32) + returned.astype(jnp.float32)).astype(jnp.bfloat16)


def solution(mesh):
    placed = (
        P("grid", "head"),
        P("grid", "head"),
        P("grid", "head"),
        P("grid", "head"),
        P(),
        P("grid", None),
        P("grid"),
    )
    return jax.shard_map(
        local, mesh=mesh, in_specs=placed, out_specs=P("grid", "head"), check_vma=False
    )
```

```python
import functools
import math

import jax
import jax.numpy as jnp
from jax import lax
from jax.experimental import pallas as pl
from jax.experimental.pallas import tpu as pltpu
from jax.sharding import PartitionSpec as P

D = 1024
HEADS = 16
BLK = 128


def halos(cells, axis):
    count = lax.axis_size(axis)
    from_left = lax.ppermute(cells, axis, [(i, i + 1) for i in range(count - 1)])
    from_right = lax.ppermute(cells, axis, [(i + 1, i) for i in range(count - 1)])
    return from_left, from_right


def attend_kernel(heads_here, head_dim, per_device, ids_ref, counts_ref, q_ref,
                  k_left, k_own, k_right, v_left, v_own, v_right,
                  o_ref, ksrc, vsrc, stacked, blockdiag, scores, running, spread, summed, sems):
    b = pl.program_id(0)
    slots = ids_ref.shape[0] // counts_ref.shape[0]
    rows, width = q_ref.shape
    scale = 1.0 / math.sqrt(head_dim)

    @pl.when(b == 0)
    def _():
        copies = []
        for s, (k_ref, v_ref) in enumerate(((k_left, v_left), (k_own, v_own), (k_right, v_right))):
            window = pl.ds(s * per_device, per_device)
            copies.append(pltpu.make_async_copy(k_ref, ksrc.at[window], sems.at[2 * s]))
            copies.append(pltpu.make_async_copy(v_ref, vsrc.at[window], sems.at[2 * s + 1]))
        for c in copies:
            c.start()
        for c in copies:
            c.wait()

    column_head = lax.broadcasted_iota(jnp.int32, (rows, width), 1) // head_dim
    q = q_ref[...]
    for h in range(heads_here):
        stacked[h * rows:(h + 1) * rows, :] = jnp.where(column_head == h, q, jnp.zeros_like(q))
    running[...] = jnp.full_like(running, -jnp.inf)
    summed[...] = jnp.zeros_like(summed)
    count = counts_ref[b]
    pairs = (count + 1) // 2

    def score_step(i, carry):
        j = 2 * i
        first = lax.dot_general(
            stacked[...], ksrc[ids_ref[b * slots + j]], (((1,), (1,)), ((), ())),
            preferred_element_type=jnp.float32,
        ) * scale
        second = lax.dot_general(
            stacked[...], ksrc[ids_ref[b * slots + j + 1]], (((1,), (1,)), ((), ())),
            preferred_element_type=jnp.float32,
        ) * scale
        second = jnp.where(j + 1 < count, second, -jnp.inf)
        scores[j] = first
        scores[j + 1] = second
        running[...] = jnp.maximum(running[...], jnp.maximum(first, second))
        return carry

    lax.fori_loop(0, pairs, score_step, 0)
    spread[...] = jnp.broadcast_to(jnp.max(running[...], axis=1, keepdims=True), spread.shape)

    def weight_step(i, acc):
        j = 2 * i
        first = jnp.exp(scores[j] - spread[...])
        second = jnp.exp(scores[j + 1] - spread[...])
        summed[...] += first + second
        parts = []
        for t, weight in enumerate((first, second)):
            low = weight.astype(jnp.bfloat16)
            parts += [low[h * rows:(h + 1) * rows, :] for h in range(heads_here)]
            v = vsrc[ids_ref[b * slots + j + t]]
            for h in range(heads_here):
                blockdiag[(t * heads_here + h) * rows:(t * heads_here + h + 1) * rows, :] = jnp.where(
                    column_head == h, v, jnp.zeros_like(v)
                )
        side = jnp.concatenate(parts, axis=1)
        return acc + jnp.dot(side, blockdiag[...], preferred_element_type=jnp.float32)

    acc = lax.fori_loop(0, pairs, weight_step, jnp.zeros((rows, width), jnp.float32))
    total = jnp.sum(summed[...], axis=1, keepdims=True)
    out = jnp.zeros((rows, width), jnp.float32)
    for h in range(heads_here):
        out = jnp.where(column_head == h, acc / total[h * rows:(h + 1) * rows, :], out)
    o_ref[...] = out.astype(o_ref.dtype)


def attend(queries, keys, values, first_block, block_lists, block_counts):
    rows, width = queries.shape
    head_dim = D // HEADS
    heads_here = width // head_dim
    per_device = keys.shape[0] // BLK
    slots = block_lists.shape[1]
    gblocks = rows // BLK
    k_left, k_right = halos(keys, "grid")
    v_left, v_right = halos(values, "grid")
    tiles = [a.reshape(per_device, BLK, width) for a in (k_left, keys, k_right, v_left, values, v_right)]
    ids = jnp.clip(block_lists - first_block, 0, 3 * per_device - 1).astype(jnp.int32)
    ids = jnp.concatenate([ids, ids[:, :1]], axis=1).reshape(-1)
    counts = block_counts.astype(jnp.int32)
    anywhere = pl.BlockSpec(memory_space=pl.ANY)
    kernel = functools.partial(attend_kernel, heads_here, head_dim, per_device)
    return pl.pallas_call(
        kernel,
        out_shape=jax.ShapeDtypeStruct((rows, width), jnp.bfloat16),
        grid_spec=pltpu.PrefetchScalarGridSpec(
            num_scalar_prefetch=2,
            grid=(gblocks,),
            in_specs=[pl.BlockSpec((BLK, width), lambda b, ids, counts: (b, 0))] + [anywhere] * 6,
            out_specs=pl.BlockSpec((BLK, width), lambda b, ids, counts: (b, 0)),
            scratch_shapes=[
                pltpu.VMEM((3 * per_device, BLK, width), jnp.bfloat16),
                pltpu.VMEM((3 * per_device, BLK, width), jnp.bfloat16),
                pltpu.VMEM((heads_here * BLK, width), jnp.bfloat16),
                pltpu.VMEM((2 * heads_here * BLK, width), jnp.bfloat16),
                pltpu.VMEM((slots + 1, heads_here * BLK, BLK), jnp.float32),
                pltpu.VMEM((heads_here * BLK, BLK), jnp.float32),
                pltpu.VMEM((heads_here * BLK, BLK), jnp.float32),
                pltpu.VMEM((heads_here * BLK, BLK), jnp.float32),
                pltpu.SemaphoreType.DMA((6,)),
            ],
        ),
        compiler_params=pltpu.CompilerParams(
            dimension_semantics=("arbitrary",),
            vmem_limit_bytes=56 * 1024 * 1024,
        ),
        cost_estimate=pl.CostEstimate(
            flops=4 * gblocks * slots * heads_here * BLK * BLK * width,
            transcendentals=gblocks * slots * heads_here * BLK * BLK,
            bytes_accessed=2 * (3 * rows * width + 6 * keys.size),
        ),
    )(ids, counts, queries, *tiles)


def local(queries, resid, keys, values, w_out, block_lists, block_counts):
    per_device = keys.shape[0] // BLK
    first_block = (lax.axis_index("grid") - 1) * per_device
    attended = attend(queries, keys, values, first_block, block_lists, block_counts)
    arrived = lax.all_to_all(attended, "head", split_axis=0, concat_axis=1, tiled=True)
    projected = jnp.dot(arrived, w_out, preferred_element_type=jnp.float32).astype(jnp.bfloat16)
    returned = lax.all_to_all(projected, "head", split_axis=1, concat_axis=0, tiled=True)
    return (resid.astype(jnp.float32) + returned.astype(jnp.float32)).astype(jnp.bfloat16)


def solution(mesh):
    placed = (
        P("grid", "head"),
        P("grid", "head"),
        P("grid", "head"),
        P("grid", "head"),
        P(),
        P("grid", None),
        P("grid"),
    )
    return jax.shard_map(
        local, mesh=mesh, in_specs=placed, out_specs=P("grid", "head"), check_vma=False
    )
```

```python
import functools
import math

import jax
import jax.numpy as jnp
from jax import lax
from jax.experimental import pallas as pl
from jax.experimental.pallas import tpu as pltpu
from jax.sharding import PartitionSpec as P

D = 1024
HEADS = 16
BLK = 128


def halos(cells, axis):
    count = lax.axis_size(axis)
    from_left = lax.ppermute(cells, axis, [(i, i + 1) for i in range(count - 1)])
    from_right = lax.ppermute(cells, axis, [(i + 1, i) for i in range(count - 1)])
    return from_left, from_right


def attend_kernel(heads_here, head_dim, per_device, ids_ref, counts_ref, q_ref,
                  k_left, k_own, k_right, v_left, v_own, v_right,
                  o_ref, ksrc, vsrc, stacked, blockdiag, scores, running, spread, summed, sems):
    b = pl.program_id(0)
    slots = ids_ref.shape[0] // counts_ref.shape[0]
    rows, width = q_ref.shape
    scale = 1.0 / math.sqrt(head_dim)

    @pl.when(b == 0)
    def _():
        copies = []
        for s, (k_ref, v_ref) in enumerate(((k_left, v_left), (k_own, v_own), (k_right, v_right))):
            window = pl.ds(s * per_device, per_device)
            copies.append(pltpu.make_async_copy(k_ref, ksrc.at[window], sems.at[2 * s]))
            copies.append(pltpu.make_async_copy(v_ref, vsrc.at[window], sems.at[2 * s + 1]))
        for c in copies:
            c.start()
        for c in copies:
            c.wait()

    column_head = lax.broadcasted_iota(jnp.int32, (rows, width), 1) // head_dim
    q = q_ref[...]
    for h in range(heads_here):
        stacked[h * rows:(h + 1) * rows, :] = jnp.where(column_head == h, q, jnp.zeros_like(q))
    running[...] = jnp.full_like(running, -jnp.inf)
    summed[...] = jnp.zeros_like(summed)
    count = counts_ref[b]
    pairs = (count + 1) // 2

    def score_step(i, carry):
        j = 2 * i
        first = lax.dot_general(
            stacked[...], ksrc[ids_ref[b * slots + j]], (((1,), (1,)), ((), ())),
            preferred_element_type=jnp.float32,
        ) * scale
        second = lax.dot_general(
            stacked[...], ksrc[ids_ref[b * slots + j + 1]], (((1,), (1,)), ((), ())),
            preferred_element_type=jnp.float32,
        ) * scale
        second = jnp.where(j + 1 < count, second, -jnp.inf)
        scores[j] = first
        scores[j + 1] = second
        running[...] = jnp.maximum(running[...], jnp.maximum(first, second))
        return carry

    lax.fori_loop(0, pairs, score_step, 0)
    spread[...] = jnp.broadcast_to(jnp.max(running[...], axis=1, keepdims=True), spread.shape)

    def weight_step(i, acc):
        j = 2 * i
        first = jnp.exp(scores[j] - spread[...])
        second = jnp.exp(scores[j + 1] - spread[...])
        summed[...] += first + second
        parts = []
        for t, weight in enumerate((first, second)):
            low = weight.astype(jnp.bfloat16)
            parts += [low[h * rows:(h + 1) * rows, :] for h in range(heads_here)]
            v = vsrc[ids_ref[b * slots + j + t]]
            for h in range(heads_here):
                blockdiag[(t * heads_here + h) * rows:(t * heads_here + h + 1) * rows, :] = jnp.where(
                    column_head == h, v, jnp.zeros_like(v)
                )
        side = jnp.concatenate(parts, axis=1)
        return acc + jnp.dot(side, blockdiag[...], preferred_element_type=jnp.float32)

    acc = lax.fori_loop(0, pairs, weight_step, jnp.zeros((rows, width), jnp.float32))
    total = jnp.sum(summed[...], axis=1, keepdims=True)
    out = jnp.zeros((rows, width), jnp.float32)
    for h in range(heads_here):
        out = jnp.where(column_head == h, acc / total[h * rows:(h + 1) * rows, :], out)
    o_ref[...] = out.astype(o_ref.dtype)


def attend(queries, keys, values, first_block, block_lists, block_counts):
    rows, width = queries.shape
    head_dim = D // HEADS
    heads_here = width // head_dim
    per_device = keys.shape[0] // BLK
    slots = block_lists.shape[1]
    gblocks = rows // BLK
    k_left, k_right = halos(keys, "grid")
    v_left, v_right = halos(values, "grid")
    tiles = [a.reshape(per_device, BLK, width) for a in (k_left, keys, k_right, v_left, values, v_right)]
    ids = jnp.clip(block_lists - first_block, 0, 3 * per_device - 1).astype(jnp.int32)
    ids = jnp.concatenate([ids, ids[:, :1]], axis=1).reshape(-1)
    counts = block_counts.astype(jnp.int32)
    anywhere = pl.BlockSpec(memory_space=pl.ANY)
    kernel = functools.partial(attend_kernel, heads_here, head_dim, per_device)
    return pl.pallas_call(
        kernel,
        out_shape=jax.ShapeDtypeStruct((rows, width), jnp.bfloat16),
        grid_spec=pltpu.PrefetchScalarGridSpec(
            num_scalar_prefetch=2,
            grid=(gblocks,),
            in_specs=[pl.BlockSpec((BLK, width), lambda b, ids, counts: (b, 0))] + [anywhere] * 6,
            out_specs=pl.BlockSpec((BLK, width), lambda b, ids, counts: (b, 0)),
            scratch_shapes=[
                pltpu.VMEM((3 * per_device, BLK, width), jnp.bfloat16),
                pltpu.VMEM((3 * per_device, BLK, width), jnp.bfloat16),
                pltpu.VMEM((heads_here * BLK, width), jnp.bfloat16),
                pltpu.VMEM((2 * heads_here * BLK, width), jnp.bfloat16),
                pltpu.VMEM((slots + 1, heads_here * BLK, BLK), jnp.float32),
                pltpu.VMEM((heads_here * BLK, BLK), jnp.float32),
                pltpu.VMEM((heads_here * BLK, BLK), jnp.float32),
                pltpu.VMEM((heads_here * BLK, BLK), jnp.float32),
                pltpu.SemaphoreType.DMA((6,)),
            ],
        ),
        compiler_params=pltpu.CompilerParams(
            dimension_semantics=("arbitrary",),
            vmem_limit_bytes=56 * 1024 * 1024,
        ),
        cost_estimate=pl.CostEstimate(
            flops=4 * gblocks * slots * heads_here * BLK * BLK * width,
            transcendentals=gblocks * slots * heads_here * BLK * BLK,
            bytes_accessed=2 * (3 * rows * width + 6 * keys.size),
        ),
    )(ids, counts, queries, *tiles)


def exchange(pieces, axis):
    count = lax.axis_size(axis)
    arrived = [pieces[0]]
    for d in range(1, count):
        arrived.append(lax.ppermute(pieces[d], axis, [(i, (i + d) % count) for i in range(count)]))
    return arrived


def project(attended, w_out, axis):
    count = lax.axis_size(axis)
    me = lax.axis_index(axis)
    rows, width = attended.shape
    share = rows // count
    chunks = attended.reshape(count, share, width)
    outgoing = [lax.dynamic_index_in_dim(chunks, (me + d) % count, 0, keepdims=False) for d in range(count)]
    incoming = exchange(outgoing, axis)
    ordered = jnp.stack(incoming)
    order = (me - jnp.arange(count)) % count
    full = jnp.zeros_like(ordered).at[order].set(ordered)
    arrived = jnp.transpose(full, (1, 0, 2)).reshape(share, count * width)
    projected = jnp.dot(arrived, w_out, preferred_element_type=jnp.float32).astype(jnp.bfloat16)
    columns = projected.reshape(share, count, width)
    back = [lax.dynamic_index_in_dim(columns, (me + d) % count, 1, keepdims=False) for d in range(count)]
    returned = exchange(back, axis)
    ordered = jnp.stack(returned)
    full = jnp.zeros_like(ordered).at[order].set(ordered)
    return full.reshape(rows, width)


def local(queries, resid, keys, values, w_out, block_lists, block_counts):
    per_device = keys.shape[0] // BLK
    first_block = (lax.axis_index("grid") - 1) * per_device
    halves = 2
    rows = queries.shape[0] // halves
    lists = block_lists.shape[0] // halves
    outputs = []
    for part in range(halves):
        attended = attend(
            queries[part * rows:(part + 1) * rows], keys, values, first_block,
            block_lists[part * lists:(part + 1) * lists], block_counts[part * lists:(part + 1) * lists],
        )
        outputs.append(project(attended, w_out, "head"))
    returned = jnp.concatenate(outputs, axis=0)
    return (resid.astype(jnp.float32) + returned.astype(jnp.float32)).astype(jnp.bfloat16)


def solution(mesh):
    placed = (
        P("grid", "head"),
        P("grid", "head"),
        P("grid", "head"),
        P("grid", "head"),
        P(),
        P("grid", None),
        P("grid"),
    )
    return jax.shard_map(
        local, mesh=mesh, in_specs=placed, out_specs=P("grid", "head"), check_vma=False
    )
```

```python
import functools
import math

import jax
import jax.numpy as jnp
from jax import lax
from jax.experimental import pallas as pl
from jax.experimental.pallas import tpu as pltpu
from jax.sharding import PartitionSpec as P

D = 1024
HEADS = 16
BLK = 128


def halos(cells, axis):
    count = lax.axis_size(axis)
    from_left = lax.ppermute(cells, axis, [(i, i + 1) for i in range(count - 1)])
    from_right = lax.ppermute(cells, axis, [(i + 1, i) for i in range(count - 1)])
    return from_left, from_right


def attend_kernel(heads_here, head_dim, per_device, ids_ref, counts_ref, q_ref,
                  k_left, k_own, k_right, v_left, v_own, v_right,
                  o_ref, ksrc, vsrc, stacked, blockdiag, scores, running, spread, summed, sems):
    b = pl.program_id(0)
    slots = ids_ref.shape[0] // counts_ref.shape[0]
    rows, width = q_ref.shape
    scale = 1.0 / math.sqrt(head_dim)

    @pl.when(b == 0)
    def _():
        copies = []
        for s, (k_ref, v_ref) in enumerate(((k_left, v_left), (k_own, v_own), (k_right, v_right))):
            window = pl.ds(s * per_device, per_device)
            copies.append(pltpu.make_async_copy(k_ref, ksrc.at[window], sems.at[2 * s]))
            copies.append(pltpu.make_async_copy(v_ref, vsrc.at[window], sems.at[2 * s + 1]))
        for c in copies:
            c.start()
        for c in copies:
            c.wait()

    column_head = lax.broadcasted_iota(jnp.int32, (rows, width), 1) // head_dim
    q = q_ref[...]
    for h in range(heads_here):
        stacked[h * rows:(h + 1) * rows, :] = jnp.where(column_head == h, q, jnp.zeros_like(q))
    running[...] = jnp.full_like(running, -jnp.inf)
    summed[...] = jnp.zeros_like(summed)
    count = counts_ref[b]
    pairs = (count + 1) // 2

    def score_step(i, carry):
        j = 2 * i
        first = lax.dot_general(
            stacked[...], ksrc[ids_ref[b * slots + j]], (((1,), (1,)), ((), ())),
            preferred_element_type=jnp.float32,
        ) * scale
        second = lax.dot_general(
            stacked[...], ksrc[ids_ref[b * slots + j + 1]], (((1,), (1,)), ((), ())),
            preferred_element_type=jnp.float32,
        ) * scale
        second = jnp.where(j + 1 < count, second, -jnp.inf)
        scores[j] = first
        scores[j + 1] = second
        running[...] = jnp.maximum(running[...], jnp.maximum(first, second))
        return carry

    lax.fori_loop(0, pairs, score_step, 0)
    spread[...] = jnp.broadcast_to(jnp.max(running[...], axis=1, keepdims=True), spread.shape)

    def weight_step(i, acc):
        j = 2 * i
        first = jnp.exp(scores[j] - spread[...])
        second = jnp.exp(scores[j + 1] - spread[...])
        summed[...] += first + second
        parts = []
        for t, weight in enumerate((first, second)):
            low = weight.astype(jnp.bfloat16)
            parts += [low[h * rows:(h + 1) * rows, :] for h in range(heads_here)]
            v = vsrc[ids_ref[b * slots + j + t]]
            for h in range(heads_here):
                blockdiag[(t * heads_here + h) * rows:(t * heads_here + h + 1) * rows, :] = jnp.where(
                    column_head == h, v, jnp.zeros_like(v)
                )
        side = jnp.concatenate(parts, axis=1)
        return acc + jnp.dot(side, blockdiag[...], preferred_element_type=jnp.float32)

    acc = lax.fori_loop(0, pairs, weight_step, jnp.zeros((rows, width), jnp.float32))
    total = jnp.sum(summed[...], axis=1, keepdims=True)
    out = jnp.zeros((rows, width), jnp.float32)
    for h in range(heads_here):
        out = jnp.where(column_head == h, acc / total[h * rows:(h + 1) * rows, :], out)
    o_ref[...] = out.astype(o_ref.dtype)


def attend(queries, keys, values, first_block, block_lists, block_counts):
    rows, width = queries.shape
    head_dim = D // HEADS
    heads_here = width // head_dim
    per_device = keys.shape[0] // BLK
    slots = block_lists.shape[1]
    gblocks = rows // BLK
    k_left, k_right = halos(keys, "grid")
    v_left, v_right = halos(values, "grid")
    tiles = [a.reshape(per_device, BLK, width) for a in (k_left, keys, k_right, v_left, values, v_right)]
    ids = jnp.clip(block_lists - first_block, 0, 3 * per_device - 1).astype(jnp.int32)
    ids = jnp.concatenate([ids, ids[:, :1]], axis=1).reshape(-1)
    counts = block_counts.astype(jnp.int32)
    anywhere = pl.BlockSpec(memory_space=pl.ANY)
    kernel = functools.partial(attend_kernel, heads_here, head_dim, per_device)
    return pl.pallas_call(
        kernel,
        out_shape=jax.ShapeDtypeStruct((rows, width), jnp.bfloat16),
        grid_spec=pltpu.PrefetchScalarGridSpec(
            num_scalar_prefetch=2,
            grid=(gblocks,),
            in_specs=[pl.BlockSpec((BLK, width), lambda b, ids, counts: (b, 0))] + [anywhere] * 6,
            out_specs=pl.BlockSpec((BLK, width), lambda b, ids, counts: (b, 0)),
            scratch_shapes=[
                pltpu.VMEM((3 * per_device, BLK, width), jnp.bfloat16),
                pltpu.VMEM((3 * per_device, BLK, width), jnp.bfloat16),
                pltpu.VMEM((heads_here * BLK, width), jnp.bfloat16),
                pltpu.VMEM((2 * heads_here * BLK, width), jnp.bfloat16),
                pltpu.VMEM((slots + 1, heads_here * BLK, BLK), jnp.float32),
                pltpu.VMEM((heads_here * BLK, BLK), jnp.float32),
                pltpu.VMEM((heads_here * BLK, BLK), jnp.float32),
                pltpu.VMEM((heads_here * BLK, BLK), jnp.float32),
                pltpu.SemaphoreType.DMA((6,)),
            ],
        ),
        compiler_params=pltpu.CompilerParams(
            dimension_semantics=("arbitrary",),
            vmem_limit_bytes=56 * 1024 * 1024,
        ),
        cost_estimate=pl.CostEstimate(
            flops=4 * gblocks * slots * heads_here * BLK * BLK * width,
            transcendentals=gblocks * slots * heads_here * BLK * BLK,
            bytes_accessed=2 * (3 * rows * width + 6 * keys.size),
        ),
    )(ids, counts, queries, *tiles)


def exchange(pieces, axis):
    count = lax.axis_size(axis)
    arrived = [pieces[0]]
    for d in range(1, count):
        arrived.append(lax.ppermute(pieces[d], axis, [(i, (i + d) % count) for i in range(count)]))
    return arrived


def permuted_weights(w_out, axis, width):
    count = lax.axis_size(axis)
    me = lax.axis_index(axis)
    rows = jnp.concatenate(
        [lax.dynamic_slice_in_dim(w_out, ((me - d) % count) * width, width, axis=0) for d in range(count)], axis=0
    )
    return jnp.concatenate(
        [lax.dynamic_slice_in_dim(rows, ((me + d) % count) * width, width, axis=1) for d in range(count)], axis=1
    )


def project(attended, weights, axis):
    count = lax.axis_size(axis)
    me = lax.axis_index(axis)
    rows, width = attended.shape
    share = rows // count
    outgoing = [lax.dynamic_slice_in_dim(attended, ((me + d) % count) * share, share, axis=0) for d in range(count)]
    incoming = exchange(outgoing, axis)
    projected = jnp.dot(
        jnp.concatenate(incoming, axis=1), weights, preferred_element_type=jnp.float32
    ).astype(jnp.bfloat16)
    back = [projected[:, d * width:(d + 1) * width] for d in range(count)]
    returned = exchange(back, axis)
    out = jnp.zeros((rows, width), jnp.bfloat16)
    for d in range(count):
        out = lax.dynamic_update_slice_in_dim(out, returned[d], ((me - d) % count) * share, axis=0)
    return out


def local(queries, resid, keys, values, w_out, block_lists, block_counts):
    per_device = keys.shape[0] // BLK
    first_block = (lax.axis_index("grid") - 1) * per_device
    weights = permuted_weights(w_out, "head", queries.shape[1])
    halves = 2
    rows = queries.shape[0] // halves
    lists = block_lists.shape[0] // halves
    outputs = []
    for part in range(halves):
        attended = attend(
            queries[part * rows:(part + 1) * rows], keys, values, first_block,
            block_lists[part * lists:(part + 1) * lists], block_counts[part * lists:(part + 1) * lists],
        )
        outputs.append(project(attended, weights, "head"))
    returned = jnp.concatenate(outputs, axis=0)
    return (resid.astype(jnp.float32) + returned.astype(jnp.float32)).astype(jnp.bfloat16)


def solution(mesh):
    placed = (
        P("grid", "head"),
        P("grid", "head"),
        P("grid", "head"),
        P("grid", "head"),
        P(),
        P("grid", None),
        P("grid"),
    )
    return jax.shard_map(
        local, mesh=mesh, in_specs=placed, out_specs=P("grid", "head"), check_vma=False
    )
```

```python
import functools
import math

import jax
import jax.numpy as jnp
from jax import lax
from jax.experimental import pallas as pl
from jax.experimental.pallas import tpu as pltpu
from jax.sharding import PartitionSpec as P

D = 1024
HEADS = 16
BLK = 128


def halos(cells, axis):
    count = lax.axis_size(axis)
    from_left = lax.ppermute(cells, axis, [(i, i + 1) for i in range(count - 1)])
    from_right = lax.ppermute(cells, axis, [(i + 1, i) for i in range(count - 1)])
    return from_left, from_right


def attend_kernel(heads_here, head_dim, per_device, ids_ref, counts_ref, q_ref,
                  k_left, k_own, k_right, v_left, v_own, v_right,
                  o_ref, ksrc, vsrc, stacked, blockdiag, scores, running, spread, summed, sems):
    b = pl.program_id(0)
    slots = ids_ref.shape[0] // counts_ref.shape[0]
    rows, width = q_ref.shape
    scale = 1.0 / math.sqrt(head_dim)

    @pl.when(b == 0)
    def _():
        copies = []
        for s, (k_ref, v_ref) in enumerate(((k_left, v_left), (k_own, v_own), (k_right, v_right))):
            window = pl.ds(s * per_device, per_device)
            copies.append(pltpu.make_async_copy(k_ref, ksrc.at[window], sems.at[2 * s]))
            copies.append(pltpu.make_async_copy(v_ref, vsrc.at[window], sems.at[2 * s + 1]))
        for c in copies:
            c.start()
        for c in copies:
            c.wait()

    column_head = lax.broadcasted_iota(jnp.int32, (rows, width), 1) // head_dim
    q = q_ref[...]
    for h in range(heads_here):
        stacked[h * rows:(h + 1) * rows, :] = jnp.where(column_head == h, q, jnp.zeros_like(q))
    running[...] = jnp.full_like(running, -jnp.inf)
    summed[...] = jnp.zeros_like(summed)
    count = counts_ref[b]
    pairs = (count + 1) // 2

    def score_step(i, carry):
        j = 2 * i
        first = lax.dot_general(
            stacked[...], ksrc[ids_ref[b * slots + j]], (((1,), (1,)), ((), ())),
            preferred_element_type=jnp.float32,
        ) * scale
        second = lax.dot_general(
            stacked[...], ksrc[ids_ref[b * slots + j + 1]], (((1,), (1,)), ((), ())),
            preferred_element_type=jnp.float32,
        ) * scale
        second = jnp.where(j + 1 < count, second, -jnp.inf)
        scores[j] = first
        scores[j + 1] = second
        running[...] = jnp.maximum(running[...], jnp.maximum(first, second))
        return carry

    lax.fori_loop(0, pairs, score_step, 0)
    spread[...] = jnp.broadcast_to(jnp.max(running[...], axis=1, keepdims=True), spread.shape)

    def weight_step(i, acc):
        j = 2 * i
        first = jnp.exp(scores[j] - spread[...])
        second = jnp.exp(scores[j + 1] - spread[...])
        summed[...] += first + second
        parts = []
        for t, weight in enumerate((first, second)):
            low = weight.astype(jnp.bfloat16)
            parts += [low[h * rows:(h + 1) * rows, :] for h in range(heads_here)]
            v = vsrc[ids_ref[b * slots + j + t]]
            for h in range(heads_here):
                blockdiag[(t * heads_here + h) * rows:(t * heads_here + h + 1) * rows, :] = jnp.where(
                    column_head == h, v, jnp.zeros_like(v)
                )
        side = jnp.concatenate(parts, axis=1)
        return acc + jnp.dot(side, blockdiag[...], preferred_element_type=jnp.float32)

    acc = lax.fori_loop(0, pairs, weight_step, jnp.zeros((rows, width), jnp.float32))
    total = jnp.sum(summed[...], axis=1, keepdims=True)
    out = jnp.zeros((rows, width), jnp.float32)
    for h in range(heads_here):
        out = jnp.where(column_head == h, acc / total[h * rows:(h + 1) * rows, :], out)
    o_ref[...] = out.astype(o_ref.dtype)


def attend(queries, keys, values, first_block, block_lists, block_counts):
    rows, width = queries.shape
    head_dim = D // HEADS
    heads_here = width // head_dim
    per_device = keys.shape[0] // BLK
    slots = block_lists.shape[1]
    gblocks = rows // BLK
    k_left, k_right = halos(keys, "grid")
    v_left, v_right = halos(values, "grid")
    tiles = [a.reshape(per_device, BLK, width) for a in (k_left, keys, k_right, v_left, values, v_right)]
    ids = jnp.clip(block_lists - first_block, 0, 3 * per_device - 1).astype(jnp.int32)
    ids = jnp.concatenate([ids, ids[:, :1]], axis=1).reshape(-1)
    counts = block_counts.astype(jnp.int32)
    anywhere = pl.BlockSpec(memory_space=pl.ANY)
    kernel = functools.partial(attend_kernel, heads_here, head_dim, per_device)
    return pl.pallas_call(
        kernel,
        out_shape=jax.ShapeDtypeStruct((rows, width), jnp.bfloat16),
        grid_spec=pltpu.PrefetchScalarGridSpec(
            num_scalar_prefetch=2,
            grid=(gblocks,),
            in_specs=[pl.BlockSpec((BLK, width), lambda b, ids, counts: (b, 0))] + [anywhere] * 6,
            out_specs=pl.BlockSpec((BLK, width), lambda b, ids, counts: (b, 0)),
            scratch_shapes=[
                pltpu.VMEM((3 * per_device, BLK, width), jnp.bfloat16),
                pltpu.VMEM((3 * per_device, BLK, width), jnp.bfloat16),
                pltpu.VMEM((heads_here * BLK, width), jnp.bfloat16),
                pltpu.VMEM((2 * heads_here * BLK, width), jnp.bfloat16),
                pltpu.VMEM((slots + 1, heads_here * BLK, BLK), jnp.float32),
                pltpu.VMEM((heads_here * BLK, BLK), jnp.float32),
                pltpu.VMEM((heads_here * BLK, BLK), jnp.float32),
                pltpu.VMEM((heads_here * BLK, BLK), jnp.float32),
                pltpu.SemaphoreType.DMA((6,)),
            ],
        ),
        compiler_params=pltpu.CompilerParams(
            dimension_semantics=("arbitrary",),
            vmem_limit_bytes=56 * 1024 * 1024,
        ),
        cost_estimate=pl.CostEstimate(
            flops=4 * gblocks * slots * heads_here * BLK * BLK * width,
            transcendentals=gblocks * slots * heads_here * BLK * BLK,
            bytes_accessed=2 * (3 * rows * width + 6 * keys.size),
        ),
    )(ids, counts, queries, *tiles)


def exchange(pieces, axis):
    count = lax.axis_size(axis)
    arrived = [pieces[0]]
    for d in range(1, count):
        arrived.append(lax.ppermute(pieces[d], axis, [(i, (i + d) % count) for i in range(count)]))
    return arrived


def permuted_weights(w_out, axis, width):
    count = lax.axis_size(axis)
    me = lax.axis_index(axis)
    rows = jnp.concatenate(
        [lax.dynamic_slice_in_dim(w_out, ((me - d) % count) * width, width, axis=0) for d in range(count)], axis=0
    )
    return jnp.concatenate(
        [lax.dynamic_slice_in_dim(rows, ((me + d) % count) * width, width, axis=1) for d in range(count)], axis=1
    )


def project(attended, weights, axis):
    count = lax.axis_size(axis)
    me = lax.axis_index(axis)
    rows, width = attended.shape
    share = rows // count
    outgoing = [lax.dynamic_slice_in_dim(attended, ((me + d) % count) * share, share, axis=0) for d in range(count)]
    incoming = exchange(outgoing, axis)
    projected = jnp.dot(
        jnp.concatenate(incoming, axis=1), weights, preferred_element_type=jnp.float32
    ).astype(jnp.bfloat16)
    back = [projected[:, d * width:(d + 1) * width] for d in range(count)]
    returned = exchange(back, axis)
    out = jnp.zeros((rows, width), jnp.bfloat16)
    for d in range(count):
        out = lax.dynamic_update_slice_in_dim(out, returned[d], ((me - d) % count) * share, axis=0)
    return out


def local(queries, resid, keys, values, w_out, block_lists, block_counts):
    per_device = keys.shape[0] // BLK
    first_block = (lax.axis_index("grid") - 1) * per_device
    weights = permuted_weights(w_out, "head", queries.shape[1])
    halves = 4
    rows = queries.shape[0] // halves
    lists = block_lists.shape[0] // halves
    outputs = []
    for part in range(halves):
        attended = attend(
            queries[part * rows:(part + 1) * rows], keys, values, first_block,
            block_lists[part * lists:(part + 1) * lists], block_counts[part * lists:(part + 1) * lists],
        )
        outputs.append(project(attended, weights, "head"))
    returned = jnp.concatenate(outputs, axis=0)
    return (resid.astype(jnp.float32) + returned.astype(jnp.float32)).astype(jnp.bfloat16)


def solution(mesh):
    placed = (
        P("grid", "head"),
        P("grid", "head"),
        P("grid", "head"),
        P("grid", "head"),
        P(),
        P("grid", None),
        P("grid"),
    )
    return jax.shard_map(
        local, mesh=mesh, in_specs=placed, out_specs=P("grid", "head"), check_vma=False
    )
```

```python
import functools
import math

import jax
import jax.numpy as jnp
from jax import lax
from jax.experimental import pallas as pl
from jax.experimental.pallas import tpu as pltpu
from jax.sharding import PartitionSpec as P

D = 1024
HEADS = 16
BLK = 128


RELAYED = (3, 4)
THROUGH = (((3, 1), (4, 0)), ((3, 7), (4, 6)))


def relayed_here(axis):
    return lax.axis_size(axis) == 8


def halos(cells, axis):
    count = lax.axis_size(axis)
    skip = RELAYED[0] if relayed_here(axis) else -1
    from_left = lax.ppermute(cells, axis, [(i, i + 1) for i in range(count - 1) if i != skip])
    from_right = lax.ppermute(cells, axis, [(i + 1, i) for i in range(count - 1) if i != skip])
    if skip < 0:
        return from_left, from_right, ()
    half = cells.shape[0] // 2
    pieces = []
    for part, pairs in enumerate(THROUGH):
        hop = lax.ppermute(cells[part * half:(part + 1) * half], axis, list(pairs))
        onward = [(via, RELAYED[1] if src == RELAYED[0] else RELAYED[0]) for src, via in pairs]
        pieces.append(lax.ppermute(hop, axis, onward))
    return from_left, from_right, tuple(pieces)


def attend_kernel(heads_here, head_dim, per_device, relay, ids_ref, counts_ref, routes_ref, q_ref,
                  k_left, k_own, k_right, v_left, v_own, v_right, *rest):
    if relay:
        k_first, k_second, v_first, v_second = rest[:4]
        rest = rest[4:]
    o_ref, ksrc, vsrc, stacked, blockdiag, scores, running, spread, summed, sems = rest
    b = pl.program_id(0)
    slots = ids_ref.shape[0] // counts_ref.shape[0]
    rows, width = q_ref.shape
    scale = 1.0 / math.sqrt(head_dim)

    def run(pairs, first_sem):
        copies = [pltpu.make_async_copy(src, dst, sems.at[first_sem + n]) for n, (src, dst) in enumerate(pairs)]
        for c in copies:
            c.start()
        for c in copies:
            c.wait()

    @pl.when(b == 0)
    def _():
        own = pl.ds(per_device, per_device)
        run(((k_own, ksrc.at[own]), (v_own, vsrc.at[own])), 0)
        for side, (k_ref, v_ref) in ((0, (k_left, v_left)), (2, (k_right, v_right))):
            window = pl.ds(side * per_device, per_device)
            if not relay:
                run(((k_ref, ksrc.at[window]), (v_ref, vsrc.at[window])), 2 + side)
                continue
            half = per_device // 2
            lower = pl.ds(side * per_device, half)
            upper = pl.ds(side * per_device + half, half)

            @pl.when(routes_ref[side // 2] == 0)
            def _():
                run(((k_ref, ksrc.at[window]), (v_ref, vsrc.at[window])), 2 + side)

            @pl.when(routes_ref[side // 2] != 0)
            def _():
                run(((k_first, ksrc.at[lower]), (k_second, ksrc.at[upper]),
                     (v_first, vsrc.at[lower]), (v_second, vsrc.at[upper])), 6 + 2 * side)

    column_head = lax.broadcasted_iota(jnp.int32, (rows, width), 1) // head_dim
    q = q_ref[...]
    for h in range(heads_here):
        stacked[h * rows:(h + 1) * rows, :] = jnp.where(column_head == h, q, jnp.zeros_like(q))
    running[...] = jnp.full_like(running, -jnp.inf)
    summed[...] = jnp.zeros_like(summed)
    count = counts_ref[b]
    pairs = (count + 1) // 2

    def score_step(i, carry):
        j = 2 * i
        first = lax.dot_general(
            stacked[...], ksrc[ids_ref[b * slots + j]], (((1,), (1,)), ((), ())),
            preferred_element_type=jnp.float32,
        ) * scale
        second = lax.dot_general(
            stacked[...], ksrc[ids_ref[b * slots + j + 1]], (((1,), (1,)), ((), ())),
            preferred_element_type=jnp.float32,
        ) * scale
        second = jnp.where(j + 1 < count, second, -jnp.inf)
        scores[j] = first
        scores[j + 1] = second
        running[...] = jnp.maximum(running[...], jnp.maximum(first, second))
        return carry

    lax.fori_loop(0, pairs, score_step, 0)
    spread[...] = jnp.broadcast_to(jnp.max(running[...], axis=1, keepdims=True), spread.shape)

    def weight_step(i, acc):
        j = 2 * i
        first = jnp.exp(scores[j] - spread[...])
        second = jnp.exp(scores[j + 1] - spread[...])
        summed[...] += first + second
        parts = []
        for t, weight in enumerate((first, second)):
            low = weight.astype(jnp.bfloat16)
            parts += [low[h * rows:(h + 1) * rows, :] for h in range(heads_here)]
            v = vsrc[ids_ref[b * slots + j + t]]
            for h in range(heads_here):
                blockdiag[(t * heads_here + h) * rows:(t * heads_here + h + 1) * rows, :] = jnp.where(
                    column_head == h, v, jnp.zeros_like(v)
                )
        side = jnp.concatenate(parts, axis=1)
        return acc + jnp.dot(side, blockdiag[...], preferred_element_type=jnp.float32)

    acc = lax.fori_loop(0, pairs, weight_step, jnp.zeros((rows, width), jnp.float32))
    total = jnp.sum(summed[...], axis=1, keepdims=True)
    out = jnp.zeros((rows, width), jnp.float32)
    for h in range(heads_here):
        out = jnp.where(column_head == h, acc / total[h * rows:(h + 1) * rows, :], out)
    o_ref[...] = out.astype(o_ref.dtype)


def attend(queries, keys, values, sources, routes, first_block, block_lists, block_counts):
    rows, width = queries.shape
    head_dim = D // HEADS
    heads_here = width // head_dim
    per_device = keys.shape[0] // BLK
    slots = block_lists.shape[1]
    gblocks = rows // BLK
    (k_left, k_right, k_relay), (v_left, v_right, v_relay) = sources
    relay = len(k_relay) > 0
    tiles = [a.reshape(per_device, BLK, width) for a in (k_left, keys, k_right, v_left, values, v_right)]
    tiles += [a.reshape(per_device // 2, BLK, width) for a in k_relay + v_relay]
    ids = jnp.clip(block_lists - first_block, 0, 3 * per_device - 1).astype(jnp.int32)
    ids = jnp.concatenate([ids, ids[:, :1]], axis=1).reshape(-1)
    counts = block_counts.astype(jnp.int32)
    anywhere = pl.BlockSpec(memory_space=pl.ANY)
    kernel = functools.partial(attend_kernel, heads_here, head_dim, per_device, relay)
    return pl.pallas_call(
        kernel,
        out_shape=jax.ShapeDtypeStruct((rows, width), jnp.bfloat16),
        grid_spec=pltpu.PrefetchScalarGridSpec(
            num_scalar_prefetch=3,
            grid=(gblocks,),
            in_specs=[pl.BlockSpec((BLK, width), lambda b, ids, counts, routes: (b, 0))] + [anywhere] * len(tiles),
            out_specs=pl.BlockSpec((BLK, width), lambda b, ids, counts, routes: (b, 0)),
            scratch_shapes=[
                pltpu.VMEM((3 * per_device, BLK, width), jnp.bfloat16),
                pltpu.VMEM((3 * per_device, BLK, width), jnp.bfloat16),
                pltpu.VMEM((heads_here * BLK, width), jnp.bfloat16),
                pltpu.VMEM((2 * heads_here * BLK, width), jnp.bfloat16),
                pltpu.VMEM((slots + 1, heads_here * BLK, BLK), jnp.float32),
                pltpu.VMEM((heads_here * BLK, BLK), jnp.float32),
                pltpu.VMEM((heads_here * BLK, BLK), jnp.float32),
                pltpu.VMEM((heads_here * BLK, BLK), jnp.float32),
                pltpu.SemaphoreType.DMA((14,)),
            ],
        ),
        compiler_params=pltpu.CompilerParams(
            dimension_semantics=("arbitrary",),
            vmem_limit_bytes=56 * 1024 * 1024,
        ),
        cost_estimate=pl.CostEstimate(
            flops=4 * gblocks * slots * heads_here * BLK * BLK * width,
            transcendentals=gblocks * slots * heads_here * BLK * BLK,
            bytes_accessed=2 * (3 * rows * width + 6 * keys.size),
        ),
    )(ids, counts, routes, queries, *tiles)


def exchange(pieces, axis):
    count = lax.axis_size(axis)
    arrived = [pieces[0]]
    for d in range(1, count):
        arrived.append(lax.ppermute(pieces[d], axis, [(i, (i + d) % count) for i in range(count)]))
    return arrived


def permuted_weights(w_out, axis, width):
    count = lax.axis_size(axis)
    me = lax.axis_index(axis)
    rows = jnp.concatenate(
        [lax.dynamic_slice_in_dim(w_out, ((me - d) % count) * width, width, axis=0) for d in range(count)], axis=0
    )
    return jnp.concatenate(
        [lax.dynamic_slice_in_dim(rows, ((me + d) % count) * width, width, axis=1) for d in range(count)], axis=1
    )


def project(attended, weights, axis):
    count = lax.axis_size(axis)
    me = lax.axis_index(axis)
    rows, width = attended.shape
    share = rows // count
    outgoing = [lax.dynamic_slice_in_dim(attended, ((me + d) % count) * share, share, axis=0) for d in range(count)]
    incoming = exchange(outgoing, axis)
    projected = jnp.dot(
        jnp.concatenate(incoming, axis=1), weights, preferred_element_type=jnp.float32
    ).astype(jnp.bfloat16)
    back = [projected[:, d * width:(d + 1) * width] for d in range(count)]
    returned = exchange(back, axis)
    out = jnp.zeros((rows, width), jnp.bfloat16)
    for d in range(count):
        out = lax.dynamic_update_slice_in_dim(out, returned[d], ((me - d) % count) * share, axis=0)
    return out


def local(queries, resid, keys, values, w_out, block_lists, block_counts):
    per_device = keys.shape[0] // BLK
    first_block = (lax.axis_index("grid") - 1) * per_device
    weights = permuted_weights(w_out, "head", queries.shape[1])
    sources = (halos(keys, "grid"), halos(values, "grid"))
    me = lax.axis_index("grid")
    routes = jnp.stack([me == RELAYED[1], me == RELAYED[0]]).astype(jnp.int32)
    halves = 2
    rows = queries.shape[0] // halves
    lists = block_lists.shape[0] // halves
    outputs = []
    for part in range(halves):
        attended = attend(
            queries[part * rows:(part + 1) * rows], keys, values, sources, routes, first_block,
            block_lists[part * lists:(part + 1) * lists], block_counts[part * lists:(part + 1) * lists],
        )
        outputs.append(project(attended, weights, "head"))
    returned = jnp.concatenate(outputs, axis=0)
    return (resid.astype(jnp.float32) + returned.astype(jnp.float32)).astype(jnp.bfloat16)


def solution(mesh):
    placed = (
        P("grid", "head"),
        P("grid", "head"),
        P("grid", "head"),
        P("grid", "head"),
        P(),
        P("grid", None),
        P("grid"),
    )
    return jax.shard_map(
        local, mesh=mesh, in_specs=placed, out_specs=P("grid", "head"), check_vma=False
    )
```

```python
import functools
import math

import jax
import jax.numpy as jnp
from jax import lax
from jax.experimental import pallas as pl
from jax.experimental.pallas import tpu as pltpu
from jax.sharding import PartitionSpec as P

D = 1024
HEADS = 16
BLK = 128


RELAYED = (3, 4)
THROUGH = (((3, 1), (4, 0)), ((3, 7), (4, 6)))


def relayed_here(axis):
    return lax.axis_size(axis) == 8


def halos(cells, axis):
    count = lax.axis_size(axis)
    skip = RELAYED[0] if relayed_here(axis) else -1
    from_left = lax.ppermute(cells, axis, [(i, i + 1) for i in range(count - 1) if i != skip])
    from_right = lax.ppermute(cells, axis, [(i + 1, i) for i in range(count - 1) if i != skip])
    if skip < 0:
        return from_left, from_right, ()
    half = cells.shape[0] // 2
    pieces = []
    for part, pairs in enumerate(THROUGH):
        hop = lax.ppermute(cells[part * half:(part + 1) * half], axis, list(pairs))
        onward = [(via, RELAYED[1] if src == RELAYED[0] else RELAYED[0]) for src, via in pairs]
        pieces.append(lax.ppermute(hop, axis, onward))
    return from_left, from_right, tuple(pieces)


def attend_kernel(heads_here, head_dim, per_device, windows, merge, ids_ref, starts_ref, lens_ref, routes_ref,
                  q_ref, *refs):
    refs = list(refs)
    if merge:
        acc_in, top_in, total_in = refs[:3]
        refs = refs[3:]
    sources = [refs.pop(0) for _ in range(2 * len(windows))]
    relay = len(refs) > 12
    if relay:
        k_first, k_second, v_first, v_second = [refs.pop(0) for _ in range(4)]
    if merge:
        o_ref = refs.pop(0)
    else:
        acc_out, top_out, total_out = [refs.pop(0) for _ in range(3)]
    ksrc, vsrc, stacked, blockdiag, scores, running, spread, summed, sems = refs
    b = pl.program_id(0)
    slots = ids_ref.shape[0] // lens_ref.shape[0]
    rows, width = q_ref.shape
    scale = 1.0 / math.sqrt(head_dim)

    def run(pairs, first_sem):
        copies = [pltpu.make_async_copy(src, dst, sems.at[first_sem + n]) for n, (src, dst) in enumerate(pairs)]
        for c in copies:
            c.start()
        for c in copies:
            c.wait()

    @pl.when(b == 0)
    def _():
        for n, side in enumerate(windows):
            k_ref, v_ref = sources[2 * n], sources[2 * n + 1]
            window = pl.ds(side * per_device, per_device)
            if not relay or side == 1:
                run(((k_ref, ksrc.at[window]), (v_ref, vsrc.at[window])), 2 * side)
                continue
            half = per_device // 2
            lower = pl.ds(side * per_device, half)
            upper = pl.ds(side * per_device + half, half)

            @pl.when(routes_ref[side // 2] == 0)
            def _():
                run(((k_ref, ksrc.at[window]), (v_ref, vsrc.at[window])), 2 * side)

            @pl.when(routes_ref[side // 2] != 0)
            def _():
                run(((k_first, ksrc.at[lower]), (k_second, ksrc.at[upper]),
                     (v_first, vsrc.at[lower]), (v_second, vsrc.at[upper])), 6 + 2 * side)

    column_head = lax.broadcasted_iota(jnp.int32, (rows, width), 1) // head_dim
    q = q_ref[...]
    for h in range(heads_here):
        stacked[h * rows:(h + 1) * rows, :] = jnp.where(column_head == h, q, jnp.zeros_like(q))
    running[...] = jnp.full_like(running, -jnp.inf)
    summed[...] = jnp.zeros_like(summed)
    first_slot = starts_ref[b]
    count = lens_ref[b]
    last_slot = first_slot + count - 1
    pairs = (count + 1) // 2

    def slot_id(j):
        return ids_ref[b * slots + jnp.minimum(first_slot + j, last_slot)]

    def score_step(i, carry):
        j = 2 * i
        first = lax.dot_general(
            stacked[...], ksrc[slot_id(j)], (((1,), (1,)), ((), ())),
            preferred_element_type=jnp.float32,
        ) * scale
        second = lax.dot_general(
            stacked[...], ksrc[slot_id(j + 1)], (((1,), (1,)), ((), ())),
            preferred_element_type=jnp.float32,
        ) * scale
        second = jnp.where(j + 1 < count, second, -jnp.inf)
        scores[j] = first
        scores[j + 1] = second
        running[...] = jnp.maximum(running[...], jnp.maximum(first, second))
        return carry

    lax.fori_loop(0, pairs, score_step, 0)
    top = jnp.max(running[...], axis=1, keepdims=True)
    spread[...] = jnp.broadcast_to(top, spread.shape)

    def weight_step(i, acc):
        j = 2 * i
        first = jnp.exp(scores[j] - spread[...])
        second = jnp.exp(scores[j + 1] - spread[...])
        summed[...] += first + second
        parts = []
        for t, weight in enumerate((first, second)):
            low = weight.astype(jnp.bfloat16)
            parts += [low[h * rows:(h + 1) * rows, :] for h in range(heads_here)]
            v = vsrc[slot_id(j + t)]
            for h in range(heads_here):
                blockdiag[(t * heads_here + h) * rows:(t * heads_here + h + 1) * rows, :] = jnp.where(
                    column_head == h, v, jnp.zeros_like(v)
                )
        side = jnp.concatenate(parts, axis=1)
        return acc + jnp.dot(side, blockdiag[...], preferred_element_type=jnp.float32)

    acc = lax.fori_loop(0, pairs, weight_step, jnp.zeros((rows, width), jnp.float32))
    total = jnp.sum(summed[...], axis=1, keepdims=True)
    top_cols = jnp.zeros((rows, width), jnp.float32)
    total_cols = jnp.zeros((rows, width), jnp.float32)
    for h in range(heads_here):
        here = column_head == h
        top_cols = jnp.where(here, top[h * rows:(h + 1) * rows, :], top_cols)
        total_cols = jnp.where(here, total[h * rows:(h + 1) * rows, :], total_cols)
    if not merge:
        acc_out[...] = acc
        top_out[...] = top_cols
        total_out[...] = total_cols
        return
    other_top = top_in[...]
    both = jnp.maximum(other_top, top_cols)
    mine = jnp.exp(top_cols - both)
    theirs = jnp.exp(other_top - both)
    out = (acc * mine + acc_in[...] * theirs) / (total_cols * mine + total_in[...] * theirs)
    o_ref[...] = out.astype(o_ref.dtype)


def attend(queries, tiles, windows, routes, ids, starts, lens, carried):
    rows, width = queries.shape
    head_dim = D // HEADS
    heads_here = width // head_dim
    per_device = tiles[0].shape[0]
    slots = ids.shape[0] // lens.shape[0]
    gblocks = rows // BLK
    merge = carried is not None
    block = pl.BlockSpec((BLK, width), lambda b, *_: (b, 0))
    anywhere = pl.BlockSpec(memory_space=pl.ANY)
    kernel = functools.partial(attend_kernel, heads_here, head_dim, per_device, tuple(windows), merge)
    if merge:
        out_shape = jax.ShapeDtypeStruct((rows, width), jnp.bfloat16)
        out_specs = block
    else:
        out_shape = [jax.ShapeDtypeStruct((rows, width), jnp.float32)] * 3
        out_specs = [block] * 3
    carried = list(carried) if merge else []
    return pl.pallas_call(
        kernel,
        out_shape=out_shape,
        grid_spec=pltpu.PrefetchScalarGridSpec(
            num_scalar_prefetch=4,
            grid=(gblocks,),
            in_specs=[block] * (1 + len(carried)) + [anywhere] * len(tiles),
            out_specs=out_specs,
            scratch_shapes=[
                pltpu.VMEM((3 * per_device, BLK, width), jnp.bfloat16),
                pltpu.VMEM((3 * per_device, BLK, width), jnp.bfloat16),
                pltpu.VMEM((heads_here * BLK, width), jnp.bfloat16),
                pltpu.VMEM((2 * heads_here * BLK, width), jnp.bfloat16),
                pltpu.VMEM((slots + 1, heads_here * BLK, BLK), jnp.float32),
                pltpu.VMEM((heads_here * BLK, BLK), jnp.float32),
                pltpu.VMEM((heads_here * BLK, BLK), jnp.float32),
                pltpu.VMEM((heads_here * BLK, BLK), jnp.float32),
                pltpu.SemaphoreType.DMA((14,)),
            ],
        ),
        compiler_params=pltpu.CompilerParams(
            dimension_semantics=("arbitrary",),
            vmem_limit_bytes=56 * 1024 * 1024,
        ),
        cost_estimate=pl.CostEstimate(
            flops=2 * gblocks * slots * heads_here * BLK * BLK * width,
            transcendentals=gblocks * slots * heads_here * BLK * BLK // 2,
            bytes_accessed=2 * 3 * rows * width + sum(t.size * 2 for t in tiles),
        ),
    )(ids, starts, lens, routes, queries, *carried, *tiles)


def exchange(pieces, axis):
    count = lax.axis_size(axis)
    arrived = [pieces[0]]
    for d in range(1, count):
        arrived.append(lax.ppermute(pieces[d], axis, [(i, (i + d) % count) for i in range(count)]))
    return arrived


def permuted_weights(w_out, axis, width):
    count = lax.axis_size(axis)
    me = lax.axis_index(axis)
    rows = jnp.concatenate(
        [lax.dynamic_slice_in_dim(w_out, ((me - d) % count) * width, width, axis=0) for d in range(count)], axis=0
    )
    return jnp.concatenate(
        [lax.dynamic_slice_in_dim(rows, ((me + d) % count) * width, width, axis=1) for d in range(count)], axis=1
    )


def project(attended, weights, axis):
    count = lax.axis_size(axis)
    me = lax.axis_index(axis)
    rows, width = attended.shape
    share = rows // count
    outgoing = [lax.dynamic_slice_in_dim(attended, ((me + d) % count) * share, share, axis=0) for d in range(count)]
    incoming = exchange(outgoing, axis)
    projected = jnp.dot(
        jnp.concatenate(incoming, axis=1), weights, preferred_element_type=jnp.float32
    ).astype(jnp.bfloat16)
    back = [projected[:, d * width:(d + 1) * width] for d in range(count)]
    returned = exchange(back, axis)
    out = jnp.zeros((rows, width), jnp.bfloat16)
    for d in range(count):
        out = lax.dynamic_update_slice_in_dim(out, returned[d], ((me - d) % count) * share, axis=0)
    return out


def local(queries, resid, keys, values, w_out, block_lists, block_counts):
    rows, width = queries.shape
    per_device = keys.shape[0] // BLK
    slots = block_lists.shape[1]
    first_block = (lax.axis_index("grid") - 1) * per_device
    weights = permuted_weights(w_out, "head", width)
    (k_left, k_right, k_relay), (v_left, v_right, v_relay) = halos(keys, "grid"), halos(values, "grid")
    me = lax.axis_index("grid")
    routes = jnp.stack([me == RELAYED[1], me == RELAYED[0]]).astype(jnp.int32)
    tile = lambda a: a.reshape(-1, BLK, width)
    own_tiles = [tile(keys), tile(values)]
    halo_tiles = [tile(k_left), tile(v_left), tile(k_right), tile(v_right)] + [tile(a) for a in k_relay + v_relay]

    ids = jnp.clip(block_lists - first_block, 0, 3 * per_device - 1).astype(jnp.int32)
    used = jnp.arange(slots, dtype=jnp.int32)[None, :] < block_counts[:, None]
    own = used & (ids // per_device == 1)
    rank = jnp.where(own, 0, jnp.where(used, 1, 2))
    order = jnp.argsort(rank, axis=1, stable=True)
    ids = jnp.take_along_axis(ids, order, axis=1)
    ids = jnp.concatenate([ids, ids[:, :1]], axis=1)
    own_count = jnp.sum(own, axis=1).astype(jnp.int32)
    halo_count = block_counts.astype(jnp.int32) - own_count
    zero = jnp.zeros_like(own_count)

    halves = 2
    part_rows = rows // halves
    lists = block_lists.shape[0] // halves
    cut = lambda a, p: a[p * lists:(p + 1) * lists]
    early = []
    for part in range(halves):
        q = queries[part * part_rows:(part + 1) * part_rows]
        flat = cut(ids, part).reshape(-1)
        early.append(attend(q, own_tiles, (1,), routes, flat, cut(zero, part), cut(own_count, part), None))
    outputs = []
    for part in range(halves):
        q = queries[part * part_rows:(part + 1) * part_rows]
        flat = cut(ids, part).reshape(-1)
        attended = attend(q, halo_tiles, (0, 2), routes, flat, cut(own_count, part), cut(halo_count, part), early[part])
        outputs.append(project(attended, weights, "head"))
    returned = jnp.concatenate(outputs, axis=0)
    return (resid.astype(jnp.float32) + returned.astype(jnp.float32)).astype(jnp.bfloat16)


def solution(mesh):
    placed = (
        P("grid", "head"),
        P("grid", "head"),
        P("grid", "head"),
        P("grid", "head"),
        P(),
        P("grid", None),
        P("grid"),
    )
    return jax.shard_map(
        local, mesh=mesh, in_specs=placed, out_specs=P("grid", "head"), check_vma=False
    )
```

```python
import functools
import math

import jax
import jax.numpy as jnp
from jax import lax
from jax.experimental import pallas as pl
from jax.experimental.pallas import tpu as pltpu
from jax.sharding import PartitionSpec as P

D = 1024
HEADS = 16
BLK = 128


RELAYED = (3, 4)
THROUGH = (((3, 1), (4, 0)), ((3, 7), (4, 6)))


def relayed_here(axis):
    return False


def halos(cells, axis):
    count = lax.axis_size(axis)
    skip = RELAYED[0] if relayed_here(axis) else -1
    from_left = lax.ppermute(cells, axis, [(i, i + 1) for i in range(count - 1) if i != skip])
    from_right = lax.ppermute(cells, axis, [(i + 1, i) for i in range(count - 1) if i != skip])
    if skip < 0:
        return from_left, from_right, ()
    half = cells.shape[0] // 2
    pieces = []
    for part, pairs in enumerate(THROUGH):
        hop = lax.ppermute(cells[part * half:(part + 1) * half], axis, list(pairs))
        onward = [(via, RELAYED[1] if src == RELAYED[0] else RELAYED[0]) for src, via in pairs]
        pieces.append(lax.ppermute(hop, axis, onward))
    return from_left, from_right, tuple(pieces)


def attend_kernel(heads_here, head_dim, per_device, windows, merge, ids_ref, starts_ref, lens_ref, routes_ref,
                  q_ref, *refs):
    refs = list(refs)
    if merge:
        acc_in, top_in, total_in = refs[:3]
        refs = refs[3:]
    sources = [refs.pop(0) for _ in range(2 * len(windows))]
    relay = len(refs) > 12
    if relay:
        k_first, k_second, v_first, v_second = [refs.pop(0) for _ in range(4)]
    if merge:
        o_ref = refs.pop(0)
    else:
        acc_out, top_out, total_out = [refs.pop(0) for _ in range(3)]
    ksrc, vsrc, stacked, blockdiag, scores, running, spread, summed, sems = refs
    b = pl.program_id(0)
    slots = ids_ref.shape[0] // lens_ref.shape[0]
    rows, width = q_ref.shape
    scale = 1.0 / math.sqrt(head_dim)

    def run(pairs, first_sem):
        copies = [pltpu.make_async_copy(src, dst, sems.at[first_sem + n]) for n, (src, dst) in enumerate(pairs)]
        for c in copies:
            c.start()
        for c in copies:
            c.wait()

    @pl.when(b == 0)
    def _():
        for n, side in enumerate(windows):
            k_ref, v_ref = sources[2 * n], sources[2 * n + 1]
            window = pl.ds(side * per_device, per_device)
            if not relay or side == 1:
                run(((k_ref, ksrc.at[window]), (v_ref, vsrc.at[window])), 2 * side)
                continue
            half = per_device // 2
            lower = pl.ds(side * per_device, half)
            upper = pl.ds(side * per_device + half, half)

            @pl.when(routes_ref[side // 2] == 0)
            def _():
                run(((k_ref, ksrc.at[window]), (v_ref, vsrc.at[window])), 2 * side)

            @pl.when(routes_ref[side // 2] != 0)
            def _():
                run(((k_first, ksrc.at[lower]), (k_second, ksrc.at[upper]),
                     (v_first, vsrc.at[lower]), (v_second, vsrc.at[upper])), 6 + 2 * side)

    column_head = lax.broadcasted_iota(jnp.int32, (rows, width), 1) // head_dim
    q = q_ref[...]
    for h in range(heads_here):
        stacked[h * rows:(h + 1) * rows, :] = jnp.where(column_head == h, q, jnp.zeros_like(q))
    running[...] = jnp.full_like(running, -jnp.inf)
    summed[...] = jnp.zeros_like(summed)
    first_slot = starts_ref[b]
    count = lens_ref[b]
    last_slot = first_slot + count - 1
    pairs = (count + 1) // 2

    def slot_id(j):
        return ids_ref[b * slots + jnp.minimum(first_slot + j, last_slot)]

    def score_step(i, carry):
        j = 2 * i
        first = lax.dot_general(
            stacked[...], ksrc[slot_id(j)], (((1,), (1,)), ((), ())),
            preferred_element_type=jnp.float32,
        ) * scale
        second = lax.dot_general(
            stacked[...], ksrc[slot_id(j + 1)], (((1,), (1,)), ((), ())),
            preferred_element_type=jnp.float32,
        ) * scale
        second = jnp.where(j + 1 < count, second, -jnp.inf)
        scores[j] = first
        scores[j + 1] = second
        running[...] = jnp.maximum(running[...], jnp.maximum(first, second))
        return carry

    lax.fori_loop(0, pairs, score_step, 0)
    top = jnp.max(running[...], axis=1, keepdims=True)
    spread[...] = jnp.broadcast_to(top, spread.shape)

    def weight_step(i, acc):
        j = 2 * i
        first = jnp.exp(scores[j] - spread[...])
        second = jnp.exp(scores[j + 1] - spread[...])
        summed[...] += first + second
        parts = []
        for t, weight in enumerate((first, second)):
            low = weight.astype(jnp.bfloat16)
            parts += [low[h * rows:(h + 1) * rows, :] for h in range(heads_here)]
            v = vsrc[slot_id(j + t)]
            for h in range(heads_here):
                blockdiag[(t * heads_here + h) * rows:(t * heads_here + h + 1) * rows, :] = jnp.where(
                    column_head == h, v, jnp.zeros_like(v)
                )
        side = jnp.concatenate(parts, axis=1)
        return acc + jnp.dot(side, blockdiag[...], preferred_element_type=jnp.float32)

    acc = lax.fori_loop(0, pairs, weight_step, jnp.zeros((rows, width), jnp.float32))
    total = jnp.sum(summed[...], axis=1, keepdims=True)
    top_cols = jnp.zeros((rows, width), jnp.float32)
    total_cols = jnp.zeros((rows, width), jnp.float32)
    for h in range(heads_here):
        here = column_head == h
        top_cols = jnp.where(here, top[h * rows:(h + 1) * rows, :], top_cols)
        total_cols = jnp.where(here, total[h * rows:(h + 1) * rows, :], total_cols)
    if not merge:
        acc_out[...] = acc
        top_out[...] = top_cols
        total_out[...] = total_cols
        return
    other_top = top_in[...]
    both = jnp.maximum(other_top, top_cols)
    mine = jnp.exp(top_cols - both)
    theirs = jnp.exp(other_top - both)
    out = (acc * mine + acc_in[...] * theirs) / (total_cols * mine + total_in[...] * theirs)
    o_ref[...] = out.astype(o_ref.dtype)


def attend(queries, tiles, windows, routes, ids, starts, lens, carried):
    rows, width = queries.shape
    head_dim = D // HEADS
    heads_here = width // head_dim
    per_device = tiles[0].shape[0]
    slots = ids.shape[0] // lens.shape[0]
    gblocks = rows // BLK
    merge = carried is not None
    block = pl.BlockSpec((BLK, width), lambda b, *_: (b, 0))
    anywhere = pl.BlockSpec(memory_space=pl.ANY)
    kernel = functools.partial(attend_kernel, heads_here, head_dim, per_device, tuple(windows), merge)
    if merge:
        out_shape = jax.ShapeDtypeStruct((rows, width), jnp.bfloat16)
        out_specs = block
    else:
        out_shape = [jax.ShapeDtypeStruct((rows, width), jnp.float32)] * 3
        out_specs = [block] * 3
    carried = list(carried) if merge else []
    return pl.pallas_call(
        kernel,
        out_shape=out_shape,
        grid_spec=pltpu.PrefetchScalarGridSpec(
            num_scalar_prefetch=4,
            grid=(gblocks,),
            in_specs=[block] * (1 + len(carried)) + [anywhere] * len(tiles),
            out_specs=out_specs,
            scratch_shapes=[
                pltpu.VMEM((3 * per_device, BLK, width), jnp.bfloat16),
                pltpu.VMEM((3 * per_device, BLK, width), jnp.bfloat16),
                pltpu.VMEM((heads_here * BLK, width), jnp.bfloat16),
                pltpu.VMEM((2 * heads_here * BLK, width), jnp.bfloat16),
                pltpu.VMEM((slots + 1, heads_here * BLK, BLK), jnp.float32),
                pltpu.VMEM((heads_here * BLK, BLK), jnp.float32),
                pltpu.VMEM((heads_here * BLK, BLK), jnp.float32),
                pltpu.VMEM((heads_here * BLK, BLK), jnp.float32),
                pltpu.SemaphoreType.DMA((14,)),
            ],
        ),
        compiler_params=pltpu.CompilerParams(
            dimension_semantics=("arbitrary",),
            vmem_limit_bytes=56 * 1024 * 1024,
        ),
        cost_estimate=pl.CostEstimate(
            flops=2 * gblocks * slots * heads_here * BLK * BLK * width,
            transcendentals=gblocks * slots * heads_here * BLK * BLK // 2,
            bytes_accessed=2 * 3 * rows * width + sum(t.size * 2 for t in tiles),
        ),
    )(ids, starts, lens, routes, queries, *carried, *tiles)


def exchange(pieces, axis):
    count = lax.axis_size(axis)
    arrived = [pieces[0]]
    for d in range(1, count):
        arrived.append(lax.ppermute(pieces[d], axis, [(i, (i + d) % count) for i in range(count)]))
    return arrived


def permuted_weights(w_out, axis, width):
    count = lax.axis_size(axis)
    me = lax.axis_index(axis)
    rows = jnp.concatenate(
        [lax.dynamic_slice_in_dim(w_out, ((me - d) % count) * width, width, axis=0) for d in range(count)], axis=0
    )
    return jnp.concatenate(
        [lax.dynamic_slice_in_dim(rows, ((me + d) % count) * width, width, axis=1) for d in range(count)], axis=1
    )


def project(attended, weights, axis):
    count = lax.axis_size(axis)
    me = lax.axis_index(axis)
    rows, width = attended.shape
    share = rows // count
    outgoing = [lax.dynamic_slice_in_dim(attended, ((me + d) % count) * share, share, axis=0) for d in range(count)]
    incoming = exchange(outgoing, axis)
    projected = jnp.dot(
        jnp.concatenate(incoming, axis=1), weights, preferred_element_type=jnp.float32
    ).astype(jnp.bfloat16)
    back = [projected[:, d * width:(d + 1) * width] for d in range(count)]
    returned = exchange(back, axis)
    out = jnp.zeros((rows, width), jnp.bfloat16)
    for d in range(count):
        out = lax.dynamic_update_slice_in_dim(out, returned[d], ((me - d) % count) * share, axis=0)
    return out


def local(queries, resid, keys, values, w_out, block_lists, block_counts):
    rows, width = queries.shape
    per_device = keys.shape[0] // BLK
    slots = block_lists.shape[1]
    first_block = (lax.axis_index("grid") - 1) * per_device
    weights = permuted_weights(w_out, "head", width)
    (k_left, k_right, k_relay), (v_left, v_right, v_relay) = halos(keys, "grid"), halos(values, "grid")
    me = lax.axis_index("grid")
    routes = jnp.stack([me == RELAYED[1], me == RELAYED[0]]).astype(jnp.int32)
    tile = lambda a: a.reshape(-1, BLK, width)
    own_tiles = [tile(keys), tile(values)]
    halo_tiles = [tile(k_left), tile(v_left), tile(k_right), tile(v_right)] + [tile(a) for a in k_relay + v_relay]

    ids = jnp.clip(block_lists - first_block, 0, 3 * per_device - 1).astype(jnp.int32)
    used = jnp.arange(slots, dtype=jnp.int32)[None, :] < block_counts[:, None]
    own = used & (ids // per_device == 1)
    rank = jnp.where(own, 0, jnp.where(used, 1, 2))
    order = jnp.argsort(rank, axis=1, stable=True)
    ids = jnp.take_along_axis(ids, order, axis=1)
    ids = jnp.concatenate([ids, ids[:, :1]], axis=1)
    own_count = jnp.sum(own, axis=1).astype(jnp.int32)
    halo_count = block_counts.astype(jnp.int32) - own_count
    zero = jnp.zeros_like(own_count)

    halves = 2
    part_rows = rows // halves
    lists = block_lists.shape[0] // halves
    cut = lambda a, p: a[p * lists:(p + 1) * lists]
    early = []
    for part in range(halves):
        q = queries[part * part_rows:(part + 1) * part_rows]
        flat = cut(ids, part).reshape(-1)
        early.append(attend(q, own_tiles, (1,), routes, flat, cut(zero, part), cut(own_count, part), None))
    outputs = []
    for part in range(halves):
        q = queries[part * part_rows:(part + 1) * part_rows]
        flat = cut(ids, part).reshape(-1)
        attended = attend(q, halo_tiles, (0, 2), routes, flat, cut(own_count, part), cut(halo_count, part), early[part])
        outputs.append(project(attended, weights, "head"))
    returned = jnp.concatenate(outputs, axis=0)
    return (resid.astype(jnp.float32) + returned.astype(jnp.float32)).astype(jnp.bfloat16)


def solution(mesh):
    placed = (
        P("grid", "head"),
        P("grid", "head"),
        P("grid", "head"),
        P("grid", "head"),
        P(),
        P("grid", None),
        P("grid"),
    )
    return jax.shard_map(
        local, mesh=mesh, in_specs=placed, out_specs=P("grid", "head"), check_vma=False
    )
```

```python
import functools
import math

import jax
import jax.numpy as jnp
from jax import lax
from jax.experimental import pallas as pl
from jax.experimental.pallas import tpu as pltpu
from jax.sharding import PartitionSpec as P

D = 1024
HEADS = 16
BLK = 128


RELAYED = (3, 4)
THROUGH = (((3, 1), (4, 0)), ((3, 7), (4, 6)))


def relayed_here(axis):
    return lax.axis_size(axis) == 8


def halos(cells, axis, after):
    count = lax.axis_size(axis)
    skip = RELAYED[0] if relayed_here(axis) else -1
    from_left = lax.ppermute(cells, axis, [(i, i + 1) for i in range(count - 1) if i != skip])
    from_right = lax.ppermute(cells, axis, [(i + 1, i) for i in range(count - 1) if i != skip])
    if skip < 0:
        return from_left, from_right, ()
    half = cells.shape[0] // 2
    pieces = []
    for part, pairs in enumerate(THROUGH):
        hop = lax.ppermute(cells[part * half:(part + 1) * half], axis, list(pairs))
        hop, _ = lax.optimization_barrier((hop, after))
        onward = [(via, RELAYED[1] if src == RELAYED[0] else RELAYED[0]) for src, via in pairs]
        pieces.append(lax.ppermute(hop, axis, onward))
    return from_left, from_right, tuple(pieces)


def attend_kernel(heads_here, head_dim, per_device, windows, merge, ids_ref, starts_ref, lens_ref, routes_ref,
                  q_ref, *refs):
    refs = list(refs)
    if merge:
        acc_in, top_in, total_in = refs[:3]
        refs = refs[3:]
    sources = [refs.pop(0) for _ in range(2 * len(windows))]
    relay = len(refs) > 12
    if relay:
        k_first, k_second, v_first, v_second = [refs.pop(0) for _ in range(4)]
    if merge:
        o_ref = refs.pop(0)
    else:
        acc_out, top_out, total_out = [refs.pop(0) for _ in range(3)]
    ksrc, vsrc, stacked, blockdiag, scores, running, spread, summed, sems = refs
    b = pl.program_id(0)
    slots = ids_ref.shape[0] // lens_ref.shape[0]
    rows, width = q_ref.shape
    scale = 1.0 / math.sqrt(head_dim)

    def run(pairs, first_sem):
        copies = [pltpu.make_async_copy(src, dst, sems.at[first_sem + n]) for n, (src, dst) in enumerate(pairs)]
        for c in copies:
            c.start()
        for c in copies:
            c.wait()

    @pl.when(b == 0)
    def _():
        for n, side in enumerate(windows):
            k_ref, v_ref = sources[2 * n], sources[2 * n + 1]
            window = pl.ds(side * per_device, per_device)
            if not relay or side == 1:
                run(((k_ref, ksrc.at[window]), (v_ref, vsrc.at[window])), 2 * side)
                continue
            half = per_device // 2
            lower = pl.ds(side * per_device, half)
            upper = pl.ds(side * per_device + half, half)

            @pl.when(routes_ref[side // 2] == 0)
            def _():
                run(((k_ref, ksrc.at[window]), (v_ref, vsrc.at[window])), 2 * side)

            @pl.when(routes_ref[side // 2] != 0)
            def _():
                run(((k_first, ksrc.at[lower]), (k_second, ksrc.at[upper]),
                     (v_first, vsrc.at[lower]), (v_second, vsrc.at[upper])), 6 + 2 * side)

    column_head = lax.broadcasted_iota(jnp.int32, (rows, width), 1) // head_dim
    q = q_ref[...]
    for h in range(heads_here):
        stacked[h * rows:(h + 1) * rows, :] = jnp.where(column_head == h, q, jnp.zeros_like(q))
    running[...] = jnp.full_like(running, -jnp.inf)
    summed[...] = jnp.zeros_like(summed)
    first_slot = starts_ref[b]
    count = lens_ref[b]
    last_slot = first_slot + count - 1
    pairs = (count + 1) // 2

    def slot_id(j):
        return ids_ref[b * slots + jnp.minimum(first_slot + j, last_slot)]

    def score_step(i, carry):
        j = 2 * i
        first = lax.dot_general(
            stacked[...], ksrc[slot_id(j)], (((1,), (1,)), ((), ())),
            preferred_element_type=jnp.float32,
        ) * scale
        second = lax.dot_general(
            stacked[...], ksrc[slot_id(j + 1)], (((1,), (1,)), ((), ())),
            preferred_element_type=jnp.float32,
        ) * scale
        second = jnp.where(j + 1 < count, second, -jnp.inf)
        scores[j] = first
        scores[j + 1] = second
        running[...] = jnp.maximum(running[...], jnp.maximum(first, second))
        return carry

    lax.fori_loop(0, pairs, score_step, 0)
    top = jnp.max(running[...], axis=1, keepdims=True)
    spread[...] = jnp.broadcast_to(top, spread.shape)

    def weight_step(i, acc):
        j = 2 * i
        first = jnp.exp(scores[j] - spread[...])
        second = jnp.exp(scores[j + 1] - spread[...])
        summed[...] += first + second
        parts = []
        for t, weight in enumerate((first, second)):
            low = weight.astype(jnp.bfloat16)
            parts += [low[h * rows:(h + 1) * rows, :] for h in range(heads_here)]
            v = vsrc[slot_id(j + t)]
            for h in range(heads_here):
                blockdiag[(t * heads_here + h) * rows:(t * heads_here + h + 1) * rows, :] = jnp.where(
                    column_head == h, v, jnp.zeros_like(v)
                )
        side = jnp.concatenate(parts, axis=1)
        return acc + jnp.dot(side, blockdiag[...], preferred_element_type=jnp.float32)

    acc = lax.fori_loop(0, pairs, weight_step, jnp.zeros((rows, width), jnp.float32))
    total = jnp.sum(summed[...], axis=1, keepdims=True)
    top_cols = jnp.zeros((rows, width), jnp.float32)
    total_cols = jnp.zeros((rows, width), jnp.float32)
    for h in range(heads_here):
        here = column_head == h
        top_cols = jnp.where(here, top[h * rows:(h + 1) * rows, :], top_cols)
        total_cols = jnp.where(here, total[h * rows:(h + 1) * rows, :], total_cols)
    if not merge:
        acc_out[...] = acc
        top_out[...] = top_cols
        total_out[...] = total_cols
        return
    other_top = top_in[...]
    both = jnp.maximum(other_top, top_cols)
    mine = jnp.exp(top_cols - both)
    theirs = jnp.exp(other_top - both)
    out = (acc * mine + acc_in[...] * theirs) / (total_cols * mine + total_in[...] * theirs)
    o_ref[...] = out.astype(o_ref.dtype)


def attend(queries, tiles, windows, routes, ids, starts, lens, carried):
    rows, width = queries.shape
    head_dim = D // HEADS
    heads_here = width // head_dim
    per_device = tiles[0].shape[0]
    slots = ids.shape[0] // lens.shape[0]
    gblocks = rows // BLK
    merge = carried is not None
    block = pl.BlockSpec((BLK, width), lambda b, *_: (b, 0))
    anywhere = pl.BlockSpec(memory_space=pl.ANY)
    kernel = functools.partial(attend_kernel, heads_here, head_dim, per_device, tuple(windows), merge)
    if merge:
        out_shape = jax.ShapeDtypeStruct((rows, width), jnp.bfloat16)
        out_specs = block
    else:
        out_shape = [jax.ShapeDtypeStruct((rows, width), jnp.float32)] * 3
        out_specs = [block] * 3
    carried = list(carried) if merge else []
    return pl.pallas_call(
        kernel,
        out_shape=out_shape,
        grid_spec=pltpu.PrefetchScalarGridSpec(
            num_scalar_prefetch=4,
            grid=(gblocks,),
            in_specs=[block] * (1 + len(carried)) + [anywhere] * len(tiles),
            out_specs=out_specs,
            scratch_shapes=[
                pltpu.VMEM((3 * per_device, BLK, width), jnp.bfloat16),
                pltpu.VMEM((3 * per_device, BLK, width), jnp.bfloat16),
                pltpu.VMEM((heads_here * BLK, width), jnp.bfloat16),
                pltpu.VMEM((2 * heads_here * BLK, width), jnp.bfloat16),
                pltpu.VMEM((slots + 1, heads_here * BLK, BLK), jnp.float32),
                pltpu.VMEM((heads_here * BLK, BLK), jnp.float32),
                pltpu.VMEM((heads_here * BLK, BLK), jnp.float32),
                pltpu.VMEM((heads_here * BLK, BLK), jnp.float32),
                pltpu.SemaphoreType.DMA((14,)),
            ],
        ),
        compiler_params=pltpu.CompilerParams(
            dimension_semantics=("arbitrary",),
            vmem_limit_bytes=56 * 1024 * 1024,
        ),
        cost_estimate=pl.CostEstimate(
            flops=2 * gblocks * slots * heads_here * BLK * BLK * width,
            transcendentals=gblocks * slots * heads_here * BLK * BLK // 2,
            bytes_accessed=2 * 3 * rows * width + sum(t.size * 2 for t in tiles),
        ),
    )(ids, starts, lens, routes, queries, *carried, *tiles)


def exchange(pieces, axis):
    count = lax.axis_size(axis)
    arrived = [pieces[0]]
    for d in range(1, count):
        arrived.append(lax.ppermute(pieces[d], axis, [(i, (i + d) % count) for i in range(count)]))
    return arrived


def permuted_weights(w_out, axis, width):
    count = lax.axis_size(axis)
    me = lax.axis_index(axis)
    rows = jnp.concatenate(
        [lax.dynamic_slice_in_dim(w_out, ((me - d) % count) * width, width, axis=0) for d in range(count)], axis=0
    )
    return jnp.concatenate(
        [lax.dynamic_slice_in_dim(rows, ((me + d) % count) * width, width, axis=1) for d in range(count)], axis=1
    )


def project(attended, weights, axis):
    count = lax.axis_size(axis)
    me = lax.axis_index(axis)
    rows, width = attended.shape
    share = rows // count
    outgoing = [lax.dynamic_slice_in_dim(attended, ((me + d) % count) * share, share, axis=0) for d in range(count)]
    incoming = exchange(outgoing, axis)
    projected = jnp.dot(
        jnp.concatenate(incoming, axis=1), weights, preferred_element_type=jnp.float32
    ).astype(jnp.bfloat16)
    back = [projected[:, d * width:(d + 1) * width] for d in range(count)]
    returned = exchange(back, axis)
    out = jnp.zeros((rows, width), jnp.bfloat16)
    for d in range(count):
        out = lax.dynamic_update_slice_in_dim(out, returned[d], ((me - d) % count) * share, axis=0)
    return out


def local(queries, resid, keys, values, w_out, block_lists, block_counts):
    rows, width = queries.shape
    per_device = keys.shape[0] // BLK
    slots = block_lists.shape[1]
    first_block = (lax.axis_index("grid") - 1) * per_device
    weights = permuted_weights(w_out, "head", width)
    me = lax.axis_index("grid")
    routes = jnp.stack([me == RELAYED[1], me == RELAYED[0]]).astype(jnp.int32)
    tile = lambda a: a.reshape(-1, BLK, width)
    own_tiles = [tile(keys), tile(values)]

    ids = jnp.clip(block_lists - first_block, 0, 3 * per_device - 1).astype(jnp.int32)
    used = jnp.arange(slots, dtype=jnp.int32)[None, :] < block_counts[:, None]
    own = used & (ids // per_device == 1)
    rank = jnp.where(own, 0, jnp.where(used, 1, 2))
    order = jnp.argsort(rank, axis=1, stable=True)
    ids = jnp.take_along_axis(ids, order, axis=1)
    ids = jnp.concatenate([ids, ids[:, :1]], axis=1)
    own_count = jnp.sum(own, axis=1).astype(jnp.int32)
    halo_count = block_counts.astype(jnp.int32) - own_count
    zero = jnp.zeros_like(own_count)

    halves = 2
    part_rows = rows // halves
    lists = block_lists.shape[0] // halves
    cut = lambda a, p: a[p * lists:(p + 1) * lists]
    early = []
    for part in range(halves):
        q = queries[part * part_rows:(part + 1) * part_rows]
        flat = cut(ids, part).reshape(-1)
        early.append(attend(q, own_tiles, (1,), routes, flat, cut(zero, part), cut(own_count, part), None))
    after = tuple(e[0] for e in early)
    (k_left, k_right, k_relay), (v_left, v_right, v_relay) = halos(keys, "grid", after), halos(values, "grid", after)
    halo_tiles = [tile(k_left), tile(v_left), tile(k_right), tile(v_right)] + [tile(a) for a in k_relay + v_relay]
    outputs = []
    for part in range(halves):
        q = queries[part * part_rows:(part + 1) * part_rows]
        flat = cut(ids, part).reshape(-1)
        attended = attend(q, halo_tiles, (0, 2), routes, flat, cut(own_count, part), cut(halo_count, part), early[part])
        outputs.append(project(attended, weights, "head"))
    returned = jnp.concatenate(outputs, axis=0)
    return (resid.astype(jnp.float32) + returned.astype(jnp.float32)).astype(jnp.bfloat16)


def solution(mesh):
    placed = (
        P("grid", "head"),
        P("grid", "head"),
        P("grid", "head"),
        P("grid", "head"),
        P(),
        P("grid", None),
        P("grid"),
    )
    return jax.shard_map(
        local, mesh=mesh, in_specs=placed, out_specs=P("grid", "head"), check_vma=False
    )
```

```python
import functools
import math

import jax
import jax.numpy as jnp
from jax import lax
from jax.experimental import pallas as pl
from jax.experimental.pallas import tpu as pltpu
from jax.sharding import PartitionSpec as P

D = 1024
HEADS = 16
BLK = 128


RELAYED = (3, 4)
THROUGH = (((3, 1), (4, 0)), ((3, 7), (4, 6)))


def relayed_here(axis):
    return False


def halos(cells, axis):
    count = lax.axis_size(axis)
    skip = RELAYED[0] if relayed_here(axis) else -1
    from_left = lax.ppermute(cells, axis, [(i, i + 1) for i in range(count - 1) if i != skip])
    from_right = lax.ppermute(cells, axis, [(i + 1, i) for i in range(count - 1) if i != skip])
    if skip < 0:
        return from_left, from_right, ()
    half = cells.shape[0] // 2
    pieces = []
    for part, pairs in enumerate(THROUGH):
        hop = lax.ppermute(cells[part * half:(part + 1) * half], axis, list(pairs))
        onward = [(via, RELAYED[1] if src == RELAYED[0] else RELAYED[0]) for src, via in pairs]
        pieces.append(lax.ppermute(hop, axis, onward))
    return from_left, from_right, tuple(pieces)


def attend_kernel(heads_here, head_dim, per_device, windows, merge, ids_ref, starts_ref, lens_ref, routes_ref,
                  q_ref, *refs):
    refs = list(refs)
    if merge:
        acc_in, top_in, total_in = refs[:3]
        refs = refs[3:]
    sources = [refs.pop(0) for _ in range(2 * len(windows))]
    relay = len(refs) > 12
    if relay:
        k_first, k_second, v_first, v_second = [refs.pop(0) for _ in range(4)]
    if merge:
        o_ref = refs.pop(0)
    else:
        acc_out, top_out, total_out = [refs.pop(0) for _ in range(3)]
    ksrc, vsrc, stacked, blockdiag, scores, running, spread, summed, sems = refs
    b = pl.program_id(0)
    slots = ids_ref.shape[0] // lens_ref.shape[0]
    rows, width = q_ref.shape
    scale = 1.0 / math.sqrt(head_dim)

    def run(pairs, first_sem):
        copies = [pltpu.make_async_copy(src, dst, sems.at[first_sem + n]) for n, (src, dst) in enumerate(pairs)]
        for c in copies:
            c.start()
        for c in copies:
            c.wait()

    @pl.when(b == 0)
    def _():
        for n, side in enumerate(windows):
            k_ref, v_ref = sources[2 * n], sources[2 * n + 1]
            window = pl.ds(side * per_device, per_device)
            if not relay or side == 1:
                run(((k_ref, ksrc.at[window]), (v_ref, vsrc.at[window])), 2 * side)
                continue
            half = per_device // 2
            lower = pl.ds(side * per_device, half)
            upper = pl.ds(side * per_device + half, half)

            @pl.when(routes_ref[side // 2] == 0)
            def _():
                run(((k_ref, ksrc.at[window]), (v_ref, vsrc.at[window])), 2 * side)

            @pl.when(routes_ref[side // 2] != 0)
            def _():
                run(((k_first, ksrc.at[lower]), (k_second, ksrc.at[upper]),
                     (v_first, vsrc.at[lower]), (v_second, vsrc.at[upper])), 6 + 2 * side)

    column_head = lax.broadcasted_iota(jnp.int32, (rows, width), 1) // head_dim
    q = q_ref[...]
    for h in range(heads_here):
        stacked[h * rows:(h + 1) * rows, :] = jnp.where(column_head == h, q, jnp.zeros_like(q))
    running[...] = jnp.full_like(running, -jnp.inf)
    summed[...] = jnp.zeros_like(summed)
    first_slot = starts_ref[b]
    count = lens_ref[b]
    last_slot = first_slot + count - 1
    pairs = (count + 1) // 2

    def slot_id(j):
        return ids_ref[b * slots + jnp.minimum(first_slot + j, last_slot)]

    def score_step(i, carry):
        j = 2 * i
        first = lax.dot_general(
            stacked[...], ksrc[slot_id(j)], (((1,), (1,)), ((), ())),
            preferred_element_type=jnp.float32,
        ) * scale
        second = lax.dot_general(
            stacked[...], ksrc[slot_id(j + 1)], (((1,), (1,)), ((), ())),
            preferred_element_type=jnp.float32,
        ) * scale
        second = jnp.where(j + 1 < count, second, -jnp.inf)
        scores[j] = first
        scores[j + 1] = second
        running[...] = jnp.maximum(running[...], jnp.maximum(first, second))
        return carry

    lax.fori_loop(0, pairs, score_step, 0)
    top = jnp.max(running[...], axis=1, keepdims=True)
    spread[...] = jnp.broadcast_to(top, spread.shape)

    def weight_step(i, acc):
        j = 2 * i
        first = jnp.exp(scores[j] - spread[...])
        second = jnp.exp(scores[j + 1] - spread[...])
        summed[...] += first + second
        parts = []
        for t, weight in enumerate((first, second)):
            low = weight.astype(jnp.bfloat16)
            parts += [low[h * rows:(h + 1) * rows, :] for h in range(heads_here)]
            v = vsrc[slot_id(j + t)]
            for h in range(heads_here):
                blockdiag[(t * heads_here + h) * rows:(t * heads_here + h + 1) * rows, :] = jnp.where(
                    column_head == h, v, jnp.zeros_like(v)
                )
        side = jnp.concatenate(parts, axis=1)
        return acc + jnp.dot(side, blockdiag[...], preferred_element_type=jnp.float32)

    acc = lax.fori_loop(0, pairs, weight_step, jnp.zeros((rows, width), jnp.float32))
    total = jnp.sum(summed[...], axis=1, keepdims=True)
    top_cols = jnp.zeros((rows, width), jnp.float32)
    total_cols = jnp.zeros((rows, width), jnp.float32)
    for h in range(heads_here):
        here = column_head == h
        top_cols = jnp.where(here, top[h * rows:(h + 1) * rows, :], top_cols)
        total_cols = jnp.where(here, total[h * rows:(h + 1) * rows, :], total_cols)
    if not merge:
        acc_out[...] = acc
        top_out[...] = top_cols
        total_out[...] = total_cols
        return
    other_top = top_in[...]
    both = jnp.maximum(other_top, top_cols)
    mine = jnp.exp(top_cols - both)
    theirs = jnp.exp(other_top - both)
    out = (acc * mine + acc_in[...] * theirs) / (total_cols * mine + total_in[...] * theirs)
    o_ref[...] = out.astype(o_ref.dtype)


def attend(queries, tiles, windows, routes, ids, starts, lens, carried, offset=0):
    width = queries.shape[1]
    head_dim = D // HEADS
    heads_here = width // head_dim
    per_device = tiles[0].shape[0]
    slots = ids.shape[0] // lens.shape[0]
    gblocks = lens.shape[0]
    rows = gblocks * BLK
    merge = carried is not None
    block = pl.BlockSpec((BLK, width), lambda b, *_: (b, 0))
    shifted = pl.BlockSpec((BLK, width), lambda b, *_: (b + offset, 0))
    anywhere = pl.BlockSpec(memory_space=pl.ANY)
    kernel = functools.partial(attend_kernel, heads_here, head_dim, per_device, tuple(windows), merge)
    if merge:
        out_shape = jax.ShapeDtypeStruct((rows, width), jnp.bfloat16)
        out_specs = block
    else:
        out_shape = [jax.ShapeDtypeStruct((rows, width), jnp.float32)] * 3
        out_specs = [block] * 3
    carried = list(carried) if merge else []
    return pl.pallas_call(
        kernel,
        out_shape=out_shape,
        grid_spec=pltpu.PrefetchScalarGridSpec(
            num_scalar_prefetch=4,
            grid=(gblocks,),
            in_specs=[shifted] * (1 + len(carried)) + [anywhere] * len(tiles),
            out_specs=out_specs,
            scratch_shapes=[
                pltpu.VMEM((3 * per_device, BLK, width), jnp.bfloat16),
                pltpu.VMEM((3 * per_device, BLK, width), jnp.bfloat16),
                pltpu.VMEM((heads_here * BLK, width), jnp.bfloat16),
                pltpu.VMEM((2 * heads_here * BLK, width), jnp.bfloat16),
                pltpu.VMEM((slots + 1, heads_here * BLK, BLK), jnp.float32),
                pltpu.VMEM((heads_here * BLK, BLK), jnp.float32),
                pltpu.VMEM((heads_here * BLK, BLK), jnp.float32),
                pltpu.VMEM((heads_here * BLK, BLK), jnp.float32),
                pltpu.SemaphoreType.DMA((14,)),
            ],
        ),
        compiler_params=pltpu.CompilerParams(
            dimension_semantics=("arbitrary",),
            vmem_limit_bytes=56 * 1024 * 1024,
        ),
        cost_estimate=pl.CostEstimate(
            flops=2 * gblocks * slots * heads_here * BLK * BLK * width,
            transcendentals=gblocks * slots * heads_here * BLK * BLK // 2,
            bytes_accessed=2 * 3 * rows * width + sum(t.size * 2 for t in tiles),
        ),
    )(ids, starts, lens, routes, queries, *carried, *tiles)


def exchange(pieces, axis):
    count = lax.axis_size(axis)
    arrived = [pieces[0]]
    for d in range(1, count):
        arrived.append(lax.ppermute(pieces[d], axis, [(i, (i + d) % count) for i in range(count)]))
    return arrived


def permuted_weights(w_out, axis, width):
    count = lax.axis_size(axis)
    me = lax.axis_index(axis)
    rows = jnp.concatenate(
        [lax.dynamic_slice_in_dim(w_out, ((me - d) % count) * width, width, axis=0) for d in range(count)], axis=0
    )
    return jnp.concatenate(
        [lax.dynamic_slice_in_dim(rows, ((me + d) % count) * width, width, axis=1) for d in range(count)], axis=1
    )


def project(attended, weights, axis):
    count = lax.axis_size(axis)
    me = lax.axis_index(axis)
    rows, width = attended.shape
    share = rows // count
    outgoing = [lax.dynamic_slice_in_dim(attended, ((me + d) % count) * share, share, axis=0) for d in range(count)]
    incoming = exchange(outgoing, axis)
    return jnp.dot(jnp.concatenate(incoming, axis=1), weights, preferred_element_type=jnp.float32).astype(jnp.bfloat16)


def send_back(projected, axis):
    count = lax.axis_size(axis)
    me = lax.axis_index(axis)
    share, width = projected.shape[0], projected.shape[1] // count
    rows = share * count
    back = [projected[:, d * width:(d + 1) * width] for d in range(count)]
    returned = exchange(back, axis)
    out = jnp.zeros((rows, width), jnp.bfloat16)
    for d in range(count):
        out = lax.dynamic_update_slice_in_dim(out, returned[d], ((me - d) % count) * share, axis=0)
    return out


def local(queries, resid, keys, values, w_out, block_lists, block_counts):
    rows, width = queries.shape
    per_device = keys.shape[0] // BLK
    slots = block_lists.shape[1]
    first_block = (lax.axis_index("grid") - 1) * per_device
    weights = permuted_weights(w_out, "head", width)
    me = lax.axis_index("grid")
    routes = jnp.stack([me == RELAYED[1], me == RELAYED[0]]).astype(jnp.int32)
    tile = lambda a: a.reshape(-1, BLK, width)
    own_tiles = [tile(keys), tile(values)]

    ids = jnp.clip(block_lists - first_block, 0, 3 * per_device - 1).astype(jnp.int32)
    used = jnp.arange(slots, dtype=jnp.int32)[None, :] < block_counts[:, None]
    own = used & (ids // per_device == 1)
    rank = jnp.where(own, 0, jnp.where(used, 1, 2))
    order = jnp.argsort(rank, axis=1, stable=True)
    ids = jnp.take_along_axis(ids, order, axis=1)
    ids = jnp.concatenate([ids, ids[:, :1]], axis=1)
    own_count = jnp.sum(own, axis=1).astype(jnp.int32)
    halo_count = block_counts.astype(jnp.int32) - own_count
    zero = jnp.zeros_like(own_count)

    gblocks = block_lists.shape[0]
    flat = ids.reshape(-1)
    early = attend(queries, own_tiles, (1,), routes, flat, zero, own_count, None)
    (k_left, k_right, k_relay), (v_left, v_right, v_relay) = halos(keys, "grid"), halos(values, "grid")
    halo_tiles = [tile(k_left), tile(v_left), tile(k_right), tile(v_right)] + [tile(a) for a in k_relay + v_relay]
    bounds = (0, gblocks // 2, 3 * gblocks // 4, gblocks)
    projected, outputs = [], []
    q = queries
    for part in range(3):
        lo, hi = bounds[part], bounds[part + 1]
        chunk = lambda a: a[lo:hi]
        attended = attend(
            q, halo_tiles, (0, 2), routes, chunk(ids).reshape(-1), chunk(own_count), chunk(halo_count), early,
            offset=lo,
        )
        projected.append(project(attended, weights, "head"))
        outputs.append(send_back(projected[-1], "head"))
        if part == 1:
            q, _ = lax.optimization_barrier((queries, projected[0]))
    returned = jnp.concatenate(outputs, axis=0)
    return (resid.astype(jnp.float32) + returned.astype(jnp.float32)).astype(jnp.bfloat16)


def solution(mesh):
    placed = (
        P("grid", "head"),
        P("grid", "head"),
        P("grid", "head"),
        P("grid", "head"),
        P(),
        P("grid", None),
        P("grid"),
    )
    return jax.shard_map(
        local, mesh=mesh, in_specs=placed, out_specs=P("grid", "head"), check_vma=False
    )
```

```python
import functools
import math

import jax
import jax.numpy as jnp
from jax import lax
from jax.experimental import pallas as pl
from jax.experimental.pallas import tpu as pltpu
from jax.sharding import PartitionSpec as P

D = 1024
HEADS = 16
BLK = 128


RELAYED = (3, 4)
THROUGH = (((3, 1), (4, 0)), ((3, 7), (4, 6)))


def relayed_here(axis):
    return False


def halos(cells, axis):
    count = lax.axis_size(axis)
    skip = RELAYED[0] if relayed_here(axis) else -1
    from_left = lax.ppermute(cells, axis, [(i, i + 1) for i in range(count - 1) if i != skip])
    from_right = lax.ppermute(cells, axis, [(i + 1, i) for i in range(count - 1) if i != skip])
    if skip < 0:
        return from_left, from_right, ()
    half = cells.shape[0] // 2
    pieces = []
    for part, pairs in enumerate(THROUGH):
        hop = lax.ppermute(cells[part * half:(part + 1) * half], axis, list(pairs))
        onward = [(via, RELAYED[1] if src == RELAYED[0] else RELAYED[0]) for src, via in pairs]
        pieces.append(lax.ppermute(hop, axis, onward))
    return from_left, from_right, tuple(pieces)


def attend_kernel(heads_here, head_dim, per_device, windows, merge, ids_ref, starts_ref, lens_ref, routes_ref,
                  q_ref, *refs):
    refs = list(refs)
    if merge:
        acc_in, top_in, total_in = refs[:3]
        refs = refs[3:]
    sources = [refs.pop(0) for _ in range(2 * len(windows))]
    relay = len(refs) > 12
    if relay:
        k_first, k_second, v_first, v_second = [refs.pop(0) for _ in range(4)]
    if merge:
        o_ref = refs.pop(0)
    else:
        acc_out, top_out, total_out = [refs.pop(0) for _ in range(3)]
    ksrc, vsrc, stacked, blockdiag, scores, running, spread, summed, sems = refs
    b = pl.program_id(0)
    slots = ids_ref.shape[0] // lens_ref.shape[0]
    rows, width = q_ref.shape
    scale = 1.0 / math.sqrt(head_dim)

    def run(pairs, first_sem):
        copies = [pltpu.make_async_copy(src, dst, sems.at[first_sem + n]) for n, (src, dst) in enumerate(pairs)]
        for c in copies:
            c.start()
        for c in copies:
            c.wait()

    @pl.when(b == 0)
    def _():
        for n, side in enumerate(windows):
            k_ref, v_ref = sources[2 * n], sources[2 * n + 1]
            if side < 0:
                window = pl.ds(routes_ref[-side - 1] * per_device, per_device)
                run(((k_ref, ksrc.at[window]), (v_ref, vsrc.at[window])), 2 * n)
                continue
            window = pl.ds(side * per_device, per_device)
            if not relay or side == 1:
                run(((k_ref, ksrc.at[window]), (v_ref, vsrc.at[window])), 2 * side)
                continue
            half = per_device // 2
            lower = pl.ds(side * per_device, half)
            upper = pl.ds(side * per_device + half, half)

            @pl.when(routes_ref[side // 2] == 0)
            def _():
                run(((k_ref, ksrc.at[window]), (v_ref, vsrc.at[window])), 2 * side)

            @pl.when(routes_ref[side // 2] != 0)
            def _():
                run(((k_first, ksrc.at[lower]), (k_second, ksrc.at[upper]),
                     (v_first, vsrc.at[lower]), (v_second, vsrc.at[upper])), 6 + 2 * side)

    column_head = lax.broadcasted_iota(jnp.int32, (rows, width), 1) // head_dim
    q = q_ref[...]
    for h in range(heads_here):
        stacked[h * rows:(h + 1) * rows, :] = jnp.where(column_head == h, q, jnp.zeros_like(q))
    running[...] = jnp.full_like(running, -jnp.inf)
    summed[...] = jnp.zeros_like(summed)
    first_slot = starts_ref[b]
    count = lens_ref[b]
    last_slot = first_slot + count - 1
    pairs = (count + 1) // 2

    def slot_id(j):
        return ids_ref[b * slots + jnp.minimum(first_slot + j, last_slot)]

    def score_step(i, carry):
        j = 2 * i
        first = lax.dot_general(
            stacked[...], ksrc[slot_id(j)], (((1,), (1,)), ((), ())),
            preferred_element_type=jnp.float32,
        ) * scale
        second = lax.dot_general(
            stacked[...], ksrc[slot_id(j + 1)], (((1,), (1,)), ((), ())),
            preferred_element_type=jnp.float32,
        ) * scale
        second = jnp.where(j + 1 < count, second, -jnp.inf)
        scores[j] = first
        scores[j + 1] = second
        running[...] = jnp.maximum(running[...], jnp.maximum(first, second))
        return carry

    lax.fori_loop(0, pairs, score_step, 0)
    top = jnp.max(running[...], axis=1, keepdims=True)
    spread[...] = jnp.broadcast_to(top, spread.shape)

    def weight_step(i, acc):
        j = 2 * i
        first = jnp.exp(scores[j] - spread[...])
        second = jnp.exp(scores[j + 1] - spread[...])
        summed[...] += first + second
        parts = []
        for t, weight in enumerate((first, second)):
            low = weight.astype(jnp.bfloat16)
            parts += [low[h * rows:(h + 1) * rows, :] for h in range(heads_here)]
            v = vsrc[slot_id(j + t)]
            for h in range(heads_here):
                blockdiag[(t * heads_here + h) * rows:(t * heads_here + h + 1) * rows, :] = jnp.where(
                    column_head == h, v, jnp.zeros_like(v)
                )
        side = jnp.concatenate(parts, axis=1)
        return acc + jnp.dot(side, blockdiag[...], preferred_element_type=jnp.float32)

    acc = lax.fori_loop(0, pairs, weight_step, jnp.zeros((rows, width), jnp.float32))
    total = jnp.sum(summed[...], axis=1, keepdims=True)
    top_cols = jnp.zeros((rows, width), jnp.float32)
    total_cols = jnp.zeros((rows, width), jnp.float32)
    for h in range(heads_here):
        here = column_head == h
        top_cols = jnp.where(here, top[h * rows:(h + 1) * rows, :], top_cols)
        total_cols = jnp.where(here, total[h * rows:(h + 1) * rows, :], total_cols)
    if not merge:
        acc_out[...] = acc
        top_out[...] = top_cols
        total_out[...] = total_cols
        return
    other_top = top_in[...]
    both = jnp.maximum(other_top, top_cols)
    mine = jnp.exp(top_cols - both)
    theirs = jnp.exp(other_top - both)
    out = (acc * mine + acc_in[...] * theirs) / (total_cols * mine + total_in[...] * theirs)
    o_ref[...] = out.astype(o_ref.dtype)


def attend(queries, tiles, windows, routes, ids, starts, lens, carried):
    rows, width = queries.shape
    head_dim = D // HEADS
    heads_here = width // head_dim
    per_device = tiles[0].shape[0]
    slots = ids.shape[0] // lens.shape[0]
    gblocks = rows // BLK
    merge = carried is not None
    block = pl.BlockSpec((BLK, width), lambda b, *_: (b, 0))
    anywhere = pl.BlockSpec(memory_space=pl.ANY)
    kernel = functools.partial(attend_kernel, heads_here, head_dim, per_device, tuple(windows), merge)
    if merge:
        out_shape = jax.ShapeDtypeStruct((rows, width), jnp.bfloat16)
        out_specs = block
    else:
        out_shape = [jax.ShapeDtypeStruct((rows, width), jnp.float32)] * 3
        out_specs = [block] * 3
    carried = list(carried) if merge else []
    return pl.pallas_call(
        kernel,
        out_shape=out_shape,
        grid_spec=pltpu.PrefetchScalarGridSpec(
            num_scalar_prefetch=4,
            grid=(gblocks,),
            in_specs=[block] * (1 + len(carried)) + [anywhere] * len(tiles),
            out_specs=out_specs,
            scratch_shapes=[
                pltpu.VMEM((3 * per_device, BLK, width), jnp.bfloat16),
                pltpu.VMEM((3 * per_device, BLK, width), jnp.bfloat16),
                pltpu.VMEM((heads_here * BLK, width), jnp.bfloat16),
                pltpu.VMEM((2 * heads_here * BLK, width), jnp.bfloat16),
                pltpu.VMEM((slots + 1, heads_here * BLK, BLK), jnp.float32),
                pltpu.VMEM((heads_here * BLK, BLK), jnp.float32),
                pltpu.VMEM((heads_here * BLK, BLK), jnp.float32),
                pltpu.VMEM((heads_here * BLK, BLK), jnp.float32),
                pltpu.SemaphoreType.DMA((14,)),
            ],
        ),
        compiler_params=pltpu.CompilerParams(
            dimension_semantics=("arbitrary",),
            vmem_limit_bytes=56 * 1024 * 1024,
        ),
        cost_estimate=pl.CostEstimate(
            flops=2 * gblocks * slots * heads_here * BLK * BLK * width,
            transcendentals=gblocks * slots * heads_here * BLK * BLK // 2,
            bytes_accessed=2 * 3 * rows * width + sum(t.size * 2 for t in tiles),
        ),
    )(ids, starts, lens, routes, queries, *carried, *tiles)


def exchange(pieces, axis):
    count = lax.axis_size(axis)
    arrived = [pieces[0]]
    for d in range(1, count):
        arrived.append(lax.ppermute(pieces[d], axis, [(i, (i + d) % count) for i in range(count)]))
    return arrived


def permuted_weights(w_out, axis, width):
    count = lax.axis_size(axis)
    me = lax.axis_index(axis)
    rows = jnp.concatenate(
        [lax.dynamic_slice_in_dim(w_out, ((me - d) % count) * width, width, axis=0) for d in range(count)], axis=0
    )
    return jnp.concatenate(
        [lax.dynamic_slice_in_dim(rows, ((me + d) % count) * width, width, axis=1) for d in range(count)], axis=1
    )


def project(attended, weights, axis):
    count = lax.axis_size(axis)
    me = lax.axis_index(axis)
    rows, width = attended.shape
    share = rows // count
    outgoing = [lax.dynamic_slice_in_dim(attended, ((me + d) % count) * share, share, axis=0) for d in range(count)]
    incoming = exchange(outgoing, axis)
    projected = jnp.dot(
        jnp.concatenate(incoming, axis=1), weights, preferred_element_type=jnp.float32
    ).astype(jnp.bfloat16)
    back = [projected[:, d * width:(d + 1) * width] for d in range(count)]
    returned = exchange(back, axis)
    out = jnp.zeros((rows, width), jnp.bfloat16)
    for d in range(count):
        out = lax.dynamic_update_slice_in_dim(out, returned[d], ((me - d) % count) * share, axis=0)
    return out


def local(queries, resid, keys, values, w_out, block_lists, block_counts):
    rows, width = queries.shape
    per_device = keys.shape[0] // BLK
    slots = block_lists.shape[1]
    first_block = (lax.axis_index("grid") - 1) * per_device
    weights = permuted_weights(w_out, "head", width)
    me = lax.axis_index("grid")
    count = lax.axis_size("grid")
    partner = [(i ^ 1, i) for i in range(count)]
    far = [(i - 1, i) for i in range(2, count, 2)] + [(i + 1, i) for i in range(1, count - 1, 2)]
    near_window = 2 * (1 - me % 2)
    far_window = 2 * (me % 2)
    routes = jnp.stack([near_window, far_window]).astype(jnp.int32)
    tile = lambda a: a.reshape(-1, BLK, width)
    near_tiles = [tile(keys), tile(values)] + [tile(lax.ppermute(a, "grid", partner)) for a in (keys, values)]
    far_tiles = [tile(lax.ppermute(a, "grid", far)) for a in (keys, values)]

    ids = jnp.clip(block_lists - first_block, 0, 3 * per_device - 1).astype(jnp.int32)
    used = jnp.arange(slots, dtype=jnp.int32)[None, :] < block_counts[:, None]
    window = ids // per_device
    near = used & ((window == 1) | (window == near_window))
    rank = jnp.where(near, 0, jnp.where(used, 1, 2))
    order = jnp.argsort(rank, axis=1, stable=True)
    ids = jnp.take_along_axis(ids, order, axis=1)
    ids = jnp.concatenate([ids, ids[:, :1]], axis=1)
    near_count = jnp.sum(near, axis=1).astype(jnp.int32)
    far_count = block_counts.astype(jnp.int32) - near_count
    zero = jnp.zeros_like(near_count)

    halves = 2
    part_rows = rows // halves
    lists = block_lists.shape[0] // halves
    cut = lambda a, p: a[p * lists:(p + 1) * lists]
    early = []
    for part in range(halves):
        q = queries[part * part_rows:(part + 1) * part_rows]
        flat = cut(ids, part).reshape(-1)
        early.append(attend(q, near_tiles, (1, -1), routes, flat, cut(zero, part), cut(near_count, part), None))
    early = lax.optimization_barrier(early)
    outputs = []
    for part in range(halves):
        q = queries[part * part_rows:(part + 1) * part_rows]
        flat = cut(ids, part).reshape(-1)
        attended = attend(q, far_tiles, (-2,), routes, flat, cut(near_count, part), cut(far_count, part), early[part])
        outputs.append(project(attended, weights, "head"))
    returned = jnp.concatenate(outputs, axis=0)
    return (resid.astype(jnp.float32) + returned.astype(jnp.float32)).astype(jnp.bfloat16)


def solution(mesh):
    placed = (
        P("grid", "head"),
        P("grid", "head"),
        P("grid", "head"),
        P("grid", "head"),
        P(),
        P("grid", None),
        P("grid"),
    )
    return jax.shard_map(
        local, mesh=mesh, in_specs=placed, out_specs=P("grid", "head"), check_vma=False
    )
```

```python
import functools
import math

import jax
import jax.numpy as jnp
from jax import lax
from jax.experimental import pallas as pl
from jax.experimental.pallas import tpu as pltpu
from jax.sharding import PartitionSpec as P

D = 1024
HEADS = 16
BLK = 128


RELAYED = (3, 4)
THROUGH = (((3, 1), (4, 0)), ((3, 7), (4, 6)))


def relayed_here(axis):
    return False


def halos(cells, axis):
    count = lax.axis_size(axis)
    skip = RELAYED[0] if relayed_here(axis) else -1
    from_left = lax.ppermute(cells, axis, [(i, i + 1) for i in range(count - 1) if i != skip])
    from_right = lax.ppermute(cells, axis, [(i + 1, i) for i in range(count - 1) if i != skip])
    if skip < 0:
        return from_left, from_right, ()
    half = cells.shape[0] // 2
    pieces = []
    for part, pairs in enumerate(THROUGH):
        hop = lax.ppermute(cells[part * half:(part + 1) * half], axis, list(pairs))
        onward = [(via, RELAYED[1] if src == RELAYED[0] else RELAYED[0]) for src, via in pairs]
        pieces.append(lax.ppermute(hop, axis, onward))
    return from_left, from_right, tuple(pieces)


def attend_kernel(heads_here, head_dim, per_device, windows, merge, ids_ref, starts_ref, lens_ref, routes_ref,
                  q_ref, *refs):
    refs = list(refs)
    if merge:
        acc_in, top_in, total_in = refs[:3]
        refs = refs[3:]
    sources = [refs.pop(0) for _ in range(2 * len(windows))]
    relay = len(refs) > 12
    if relay:
        k_first, k_second, v_first, v_second = [refs.pop(0) for _ in range(4)]
    if merge:
        o_ref = refs.pop(0)
    else:
        acc_out, top_out, total_out = [refs.pop(0) for _ in range(3)]
    ksrc, vsrc, stacked, blockdiag, scores, running, spread, summed, sems = refs
    b = pl.program_id(0)
    slots = ids_ref.shape[0] // lens_ref.shape[0]
    rows, width = q_ref.shape
    scale = 1.0 / math.sqrt(head_dim)

    def run(pairs, first_sem):
        copies = [pltpu.make_async_copy(src, dst, sems.at[first_sem + n]) for n, (src, dst) in enumerate(pairs)]
        for c in copies:
            c.start()
        for c in copies:
            c.wait()

    @pl.when(b == 0)
    def _():
        for n, side in enumerate(windows):
            k_ref, v_ref = sources[2 * n], sources[2 * n + 1]
            if side < 0:
                window = pl.ds(routes_ref[-side - 1] * per_device, per_device)
                run(((k_ref, ksrc.at[window]), (v_ref, vsrc.at[window])), 2 * n)
                continue
            window = pl.ds(side * per_device, per_device)
            if not relay or side == 1:
                run(((k_ref, ksrc.at[window]), (v_ref, vsrc.at[window])), 2 * side)
                continue
            half = per_device // 2
            lower = pl.ds(side * per_device, half)
            upper = pl.ds(side * per_device + half, half)

            @pl.when(routes_ref[side // 2] == 0)
            def _():
                run(((k_ref, ksrc.at[window]), (v_ref, vsrc.at[window])), 2 * side)

            @pl.when(routes_ref[side // 2] != 0)
            def _():
                run(((k_first, ksrc.at[lower]), (k_second, ksrc.at[upper]),
                     (v_first, vsrc.at[lower]), (v_second, vsrc.at[upper])), 6 + 2 * side)

    column_head = lax.broadcasted_iota(jnp.int32, (rows, width), 1) // head_dim
    q = q_ref[...]
    for h in range(heads_here):
        stacked[h * rows:(h + 1) * rows, :] = jnp.where(column_head == h, q, jnp.zeros_like(q))
    running[...] = jnp.full_like(running, -jnp.inf)
    summed[...] = jnp.zeros_like(summed)
    first_slot = starts_ref[b]
    count = lens_ref[b]
    last_slot = first_slot + count - 1
    pairs = (count + 1) // 2

    def slot_id(j):
        return ids_ref[b * slots + jnp.minimum(first_slot + j, last_slot)]

    def score_step(i, carry):
        j = 2 * i
        first = lax.dot_general(
            stacked[...], ksrc[slot_id(j)], (((1,), (1,)), ((), ())),
            preferred_element_type=jnp.float32,
        ) * scale
        second = lax.dot_general(
            stacked[...], ksrc[slot_id(j + 1)], (((1,), (1,)), ((), ())),
            preferred_element_type=jnp.float32,
        ) * scale
        second = jnp.where(j + 1 < count, second, -jnp.inf)
        scores[j] = first
        scores[j + 1] = second
        running[...] = jnp.maximum(running[...], jnp.maximum(first, second))
        return carry

    lax.fori_loop(0, pairs, score_step, 0)
    top = jnp.max(running[...], axis=1, keepdims=True)
    spread[...] = jnp.broadcast_to(top, spread.shape)

    def weight_step(i, acc):
        j = 2 * i
        first = jnp.exp(scores[j] - spread[...])
        second = jnp.exp(scores[j + 1] - spread[...])
        summed[...] += first + second
        parts = []
        for t, weight in enumerate((first, second)):
            low = weight.astype(jnp.bfloat16)
            parts += [low[h * rows:(h + 1) * rows, :] for h in range(heads_here)]
            v = vsrc[slot_id(j + t)]
            for h in range(heads_here):
                blockdiag[(t * heads_here + h) * rows:(t * heads_here + h + 1) * rows, :] = jnp.where(
                    column_head == h, v, jnp.zeros_like(v)
                )
        side = jnp.concatenate(parts, axis=1)
        return acc + jnp.dot(side, blockdiag[...], preferred_element_type=jnp.float32)

    acc = lax.fori_loop(0, pairs, weight_step, jnp.zeros((rows, width), jnp.float32))
    total = jnp.sum(summed[...], axis=1, keepdims=True)
    top_cols = jnp.zeros((rows, width), jnp.float32)
    total_cols = jnp.zeros((rows, width), jnp.float32)
    for h in range(heads_here):
        here = column_head == h
        top_cols = jnp.where(here, top[h * rows:(h + 1) * rows, :], top_cols)
        total_cols = jnp.where(here, total[h * rows:(h + 1) * rows, :], total_cols)
    if not merge:
        acc_out[...] = acc
        top_out[...] = top_cols
        total_out[...] = total_cols
        return
    other_top = top_in[...]
    both = jnp.maximum(other_top, top_cols)
    mine = jnp.exp(top_cols - both)
    theirs = jnp.exp(other_top - both)
    out = (acc * mine + acc_in[...] * theirs) / (total_cols * mine + total_in[...] * theirs)
    o_ref[...] = out.astype(o_ref.dtype)


def attend(queries, tiles, windows, routes, ids, starts, lens, carried):
    rows, width = queries.shape
    head_dim = D // HEADS
    heads_here = width // head_dim
    per_device = tiles[0].shape[0]
    slots = ids.shape[0] // lens.shape[0]
    gblocks = rows // BLK
    merge = carried is not None
    block = pl.BlockSpec((BLK, width), lambda b, *_: (b, 0))
    anywhere = pl.BlockSpec(memory_space=pl.ANY)
    kernel = functools.partial(attend_kernel, heads_here, head_dim, per_device, tuple(windows), merge)
    if merge:
        out_shape = jax.ShapeDtypeStruct((rows, width), jnp.bfloat16)
        out_specs = block
    else:
        out_shape = [jax.ShapeDtypeStruct((rows, width), jnp.float32)] * 3
        out_specs = [block] * 3
    carried = list(carried) if merge else []
    return pl.pallas_call(
        kernel,
        out_shape=out_shape,
        grid_spec=pltpu.PrefetchScalarGridSpec(
            num_scalar_prefetch=4,
            grid=(gblocks,),
            in_specs=[block] * (1 + len(carried)) + [anywhere] * len(tiles),
            out_specs=out_specs,
            scratch_shapes=[
                pltpu.VMEM((3 * per_device, BLK, width), jnp.bfloat16),
                pltpu.VMEM((3 * per_device, BLK, width), jnp.bfloat16),
                pltpu.VMEM((heads_here * BLK, width), jnp.bfloat16),
                pltpu.VMEM((2 * heads_here * BLK, width), jnp.bfloat16),
                pltpu.VMEM((slots + 1, heads_here * BLK, BLK), jnp.float32),
                pltpu.VMEM((heads_here * BLK, BLK), jnp.float32),
                pltpu.VMEM((heads_here * BLK, BLK), jnp.float32),
                pltpu.VMEM((heads_here * BLK, BLK), jnp.float32),
                pltpu.SemaphoreType.DMA((14,)),
            ],
        ),
        compiler_params=pltpu.CompilerParams(
            dimension_semantics=("arbitrary",),
            vmem_limit_bytes=56 * 1024 * 1024,
        ),
        cost_estimate=pl.CostEstimate(
            flops=2 * gblocks * slots * heads_here * BLK * BLK * width,
            transcendentals=gblocks * slots * heads_here * BLK * BLK // 2,
            bytes_accessed=2 * 3 * rows * width + sum(t.size * 2 for t in tiles),
        ),
    )(ids, starts, lens, routes, queries, *carried, *tiles)


def exchange(pieces, axis):
    count = lax.axis_size(axis)
    arrived = [pieces[0]]
    for d in range(1, count):
        arrived.append(lax.ppermute(pieces[d], axis, [(i, (i + d) % count) for i in range(count)]))
    return arrived


def permuted_weights(w_out, axis, width):
    count = lax.axis_size(axis)
    me = lax.axis_index(axis)
    rows = jnp.concatenate(
        [lax.dynamic_slice_in_dim(w_out, ((me - d) % count) * width, width, axis=0) for d in range(count)], axis=0
    )
    return jnp.concatenate(
        [lax.dynamic_slice_in_dim(rows, ((me + d) % count) * width, width, axis=1) for d in range(count)], axis=1
    )


def project(attended, weights, axis):
    count = lax.axis_size(axis)
    me = lax.axis_index(axis)
    rows, width = attended.shape
    share = rows // count
    outgoing = [lax.dynamic_slice_in_dim(attended, ((me + d) % count) * share, share, axis=0) for d in range(count)]
    incoming = exchange(outgoing, axis)
    projected = jnp.dot(
        jnp.concatenate(incoming, axis=1), weights, preferred_element_type=jnp.float32
    ).astype(jnp.bfloat16)
    back = [projected[:, d * width:(d + 1) * width] for d in range(count)]
    returned = exchange(back, axis)
    out = jnp.zeros((rows, width), jnp.bfloat16)
    for d in range(count):
        out = lax.dynamic_update_slice_in_dim(out, returned[d], ((me - d) % count) * share, axis=0)
    return out


def project_at_once(attended, w_out, axis):
    arrived = lax.all_to_all(attended, axis, split_axis=0, concat_axis=1, tiled=True)
    projected = jnp.dot(arrived, w_out, preferred_element_type=jnp.float32).astype(jnp.bfloat16)
    return lax.all_to_all(projected, axis, split_axis=1, concat_axis=0, tiled=True)


def local(queries, resid, keys, values, w_out, block_lists, block_counts):
    rows, width = queries.shape
    per_device = keys.shape[0] // BLK
    slots = block_lists.shape[1]
    first_block = (lax.axis_index("grid") - 1) * per_device
    weights = permuted_weights(w_out, "head", width)
    me = lax.axis_index("grid")
    count = lax.axis_size("grid")
    partner = [(i ^ 1, i) for i in range(count)]
    far = [(i - 1, i) for i in range(2, count, 2)] + [(i + 1, i) for i in range(1, count - 1, 2)]
    near_window = 2 * (1 - me % 2)
    far_window = 2 * (me % 2)
    routes = jnp.stack([near_window, far_window]).astype(jnp.int32)
    tile = lambda a: a.reshape(-1, BLK, width)
    near_tiles = [tile(keys), tile(values)] + [tile(lax.ppermute(a, "grid", partner)) for a in (keys, values)]
    far_tiles = [tile(lax.ppermute(a, "grid", far)) for a in (keys, values)]

    ids = jnp.clip(block_lists - first_block, 0, 3 * per_device - 1).astype(jnp.int32)
    used = jnp.arange(slots, dtype=jnp.int32)[None, :] < block_counts[:, None]
    window = ids // per_device
    near = used & ((window == 1) | (window == near_window))
    rank = jnp.where(near, 0, jnp.where(used, 1, 2))
    order = jnp.argsort(rank, axis=1, stable=True)
    ids = jnp.take_along_axis(ids, order, axis=1)
    ids = jnp.concatenate([ids, ids[:, :1]], axis=1)
    near_count = jnp.sum(near, axis=1).astype(jnp.int32)
    far_count = block_counts.astype(jnp.int32) - near_count
    zero = jnp.zeros_like(near_count)

    halves = 2
    part_rows = rows // halves
    lists = block_lists.shape[0] // halves
    cut = lambda a, p: a[p * lists:(p + 1) * lists]
    early = []
    for part in range(halves):
        q = queries[part * part_rows:(part + 1) * part_rows]
        flat = cut(ids, part).reshape(-1)
        early.append(attend(q, near_tiles, (1, -1), routes, flat, cut(zero, part), cut(near_count, part), None))
    early = lax.optimization_barrier(early)
    outputs = []
    for part in range(halves):
        q = queries[part * part_rows:(part + 1) * part_rows]
        flat = cut(ids, part).reshape(-1)
        attended = attend(q, far_tiles, (-2,), routes, flat, cut(near_count, part), cut(far_count, part), early[part])
        if part < halves - 1:
            outputs.append(project(attended, weights, "head"))
        else:
            outputs.append(project_at_once(attended, w_out, "head"))
    returned = jnp.concatenate(outputs, axis=0)
    return (resid.astype(jnp.float32) + returned.astype(jnp.float32)).astype(jnp.bfloat16)


def solution(mesh):
    placed = (
        P("grid", "head"),
        P("grid", "head"),
        P("grid", "head"),
        P("grid", "head"),
        P(),
        P("grid", None),
        P("grid"),
    )
    return jax.shard_map(
        local, mesh=mesh, in_specs=placed, out_specs=P("grid", "head"), check_vma=False
    )
```
